256 devices in a mesh: term: 8 (over y, x_hi), sector: 32 (over x_lo, z, core).
Axes of the slice: x: 4 (x_hi: 2, x_lo: 2; x = x_hi * 2 + x_lo), y: 4, z: 8, core: 2. Of those that a mesh axis runs over, the one named last changes fastest.
Arguments:
- psi: float32 [512, 128, 128], P('sector'), may hold values from -6 to 6
- left_env: float32 [32, 512, 128, 128], P('term', 'sector'), may hold values from -0.5 to 0.5
- right_env: float32 [32, 512, 128, 128], P('term', 'sector'), may hold values from -0.09375 to 0.09375
- target: int32 [32, 512], P('term', 'sector'), may hold values from 0 to 511, as said below
Outputs:
- sigma: float32 [512, 128, 128], P('sector', 'term')
The draws below stay inside these ranges and needn't reach their ends.
Inputs may be any that keep to these rules, and one draw needn't show every extreme that they name: Among the 4 * 16 pairs of terms w in one block of 4 consecutive terms and source blocks s in one block of 16 consecutive blocks, at most 4 have their target in any one block of 16 consecutive target blocks, and exactly 4 do for some such block.
All inputs are finite; a program needn't handle non-finite values.
Results may differ from the reference program's by a relative error of at most 0.0001.
Values sent between devices are 32-bit elements; how exact they have to be, the bound alone decides.
No kernel may reach another device: no remote copies, remote signals or barrier semaphores. Data moves between devices by JAX's collectives and lax.ppermute only.
A program may use at most 128 MiB of HBM per device.

```python
import jax
import jax.numpy as jnp
from jax import lax

B = 128
K_DEV = 4
S_DEV = 16
CAP = 4
K = 32
NS = 512
N_TERM = 8
N_SECTOR = 32


def draw_target(key, part):
    item_count = K_DEV * S_DEV
    device_keys = jax.random.split(key, N_TERM * N_SECTOR)

    def one_block(sub):
        key_one, key_two, key_three, key_four = jax.random.split(sub, 4)
        chosen = jax.random.randint(key_one, (), 0, N_SECTOR)
        others = jax.random.permutation(key_two, (N_SECTOR - 1) * CAP)[:item_count - CAP]
        others = jnp.where(others >= CAP * chosen, others + CAP, others)
        slots_all = jnp.concatenate([chosen * CAP + jnp.arange(CAP), others])
        slots_all = jax.random.permutation(key_three, slots_all)
        local_pick = jax.random.randint(key_four, (item_count,), 0, S_DEV)
        return slots_all // CAP * S_DEV + local_pick
    values = jax.vmap(one_block)(device_keys)
    values = values.reshape(N_TERM, N_SECTOR, K_DEV, S_DEV).transpose(0, 2, 1, 3)
    return values.reshape(K_DEV * N_TERM, S_DEV * N_SECTOR).astype(jnp.int32)


def shard_levels(own_key, shape, cuts, smallest, high):
    gain = 1.0
    for dim, blocks in cuts:
        draws = jax.random.uniform(jax.random.fold_in(jax.random.fold_in(own_key, 6), dim), (blocks,), jnp.float32, smallest / len(cuts), high / len(cuts))
        gain = gain * jnp.repeat(jnp.exp(draws), shape[dim] // blocks).reshape((-1,) + (1,) * (len(shape) - 1 - dim))
    return gain


def centred(rng, dims, width, limit, cuts=(), held_as=jnp.bfloat16):
    level = shard_levels(rng, dims, cuts, -0.22, 0.18) if cuts else 1.0
    entries = jax.random.normal(rng, dims, jnp.float32) * width * level
    return jnp.minimum(jnp.maximum(entries, -limit), limit).astype(held_as)


def setup_inputs(seed: int = 0) -> dict:
    streams_of = jax.random.split(jax.random.key(seed), 5)
    psi = centred(streams_of[0], (NS, B, B), 1.0, 6.0, ((0, 32),), jnp.float32)
    left_env = centred(streams_of[1], (K, NS, B, B), B ** -0.5, 0.5, ((0, 8), (1, 32)), jnp.float32)
    right_env = centred(streams_of[2], (K, NS, B, B), (B * K) ** -0.5, 0.09375, ((0, 8), (1, 32)), jnp.float32)
    target = draw_target(jax.random.fold_in(streams_of[4], 71), 0)
    return {"psi": psi, "left_env": left_env, "right_env": right_env, "target": target}


def reference(psi, left_env, right_env, target):
    def one_term(carry, inputs):
        left_w, right_w, target_w = inputs
        contracted = jnp.einsum('sab,sbc->sac', left_w, psi, precision=lax.Precision.HIGHEST)
        picked = right_w[target_w]
        products = jnp.einsum('sab,sbc->sac', contracted, picked, precision=lax.Precision.HIGHEST)
        summed = jax.ops.segment_sum(products, target_w, num_segments=psi.shape[0])
        return carry + summed, None

    total, unused = lax.scan(one_term, jnp.zeros(psi.shape, jnp.float32), (left_env, right_env, target))
    return total
```

```python
import jax
import jax.numpy as jnp
from jax import lax
from jax.experimental import pallas as pl
from jax.experimental.pallas import tpu as pltpu
from jax.sharding import PartitionSpec as P

CAP = 4
GROUP = 8


def slot_tables(target_part):
    term_count, sector_count = target_part.shape
    item_count = term_count * sector_count
    slot_count = lax.axis_size("sector") * CAP
    flat_target = target_part.reshape(item_count)
    owner_dev = flat_target // sector_count
    local_target = flat_target % sector_count
    item_index = jnp.arange(item_count, dtype=jnp.int32)
    term_index = item_index // sector_count
    earlier = (owner_dev[:, None] == owner_dev[None, :]) & (
        item_index[None, :] < item_index[:, None]
    )
    rank_slot = jnp.sum(earlier.astype(jnp.int32), axis=1)
    slot_index = owner_dev * CAP + rank_slot
    match = slot_index[None, :] == jnp.arange(slot_count, dtype=jnp.int32)[:, None]
    occupied = jnp.any(match, axis=1)
    item_of_slot = jnp.sum(jnp.where(match, item_index[None, :], 0), axis=1)
    label_of_item = term_index * sector_count + local_target + 1
    labels = jnp.where(occupied, label_of_item[item_of_slot], 0).astype(jnp.int32)
    return item_of_slot.astype(jnp.int32), labels


def sender_kernel(item_ref, label_ref, left_ref, psi_ref, out_ref):
    sector_count = psi_ref.shape[0]
    step = pl.program_id(0)
    for j in range(GROUP):
        slot = step * GROUP + j
        item = item_ref[slot]
        term = item // sector_count
        source = item % sector_count

        @pl.when(label_ref[slot] > 0)
        def _():
            out_ref[j] = jnp.dot(
                left_ref[term, source],
                psi_ref[source],
                precision=lax.Precision.HIGHEST,
                preferred_element_type=jnp.float32,
            )

        @pl.when(label_ref[slot] == 0)
        def _():
            out_ref[j] = jnp.zeros(out_ref.shape[1:], jnp.float32)


def send_blocks(item_of_slot, labels, left_env, psi):
    slot_count = item_of_slot.shape[0]
    width = psi.shape[-1]
    grid_spec = pltpu.PrefetchScalarGridSpec(
        num_scalar_prefetch=2,
        grid=(slot_count // GROUP,),
        in_specs=[
            pl.BlockSpec(left_env.shape, lambda g, *_: (0, 0, 0, 0)),
            pl.BlockSpec(psi.shape, lambda g, *_: (0, 0, 0)),
        ],
        out_specs=pl.BlockSpec((GROUP, width, width), lambda g, *_: (g, 0, 0)),
    )
    return pl.pallas_call(
        sender_kernel,
        grid_spec=grid_spec,
        out_shape=jax.ShapeDtypeStruct((slot_count, width, width), jnp.float32),
        compiler_params=pltpu.CompilerParams(vmem_limit_bytes=48 * 1024 * 1024),
    )(item_of_slot, labels, left_env, psi)


def receiver_kernel(label_ref, incoming_ref, right_ref, out_ref):
    sector_count = out_ref.shape[0]
    step = pl.program_id(0)

    @pl.when(step == 0)
    def _():
        out_ref[...] = jnp.zeros(out_ref.shape, jnp.float32)

    for j in range(GROUP):
        label = label_ref[step * GROUP + j]

        @pl.when(label > 0)
        def _():
            pair = label - 1
            term = pair // sector_count
            tgt = pair % sector_count
            out_ref[tgt] += jnp.dot(
                incoming_ref[j],
                right_ref[term, tgt],
                precision=lax.Precision.HIGHEST,
                preferred_element_type=jnp.float32,
            )


def receive_blocks(labels, incoming, right_env):
    slot_count = labels.shape[0]
    sector_count = right_env.shape[1]
    width = right_env.shape[-1]
    grid_spec = pltpu.PrefetchScalarGridSpec(
        num_scalar_prefetch=1,
        grid=(slot_count // GROUP,),
        in_specs=[
            pl.BlockSpec((GROUP, width, width), lambda g, *_: (g, 0, 0)),
            pl.BlockSpec(right_env.shape, lambda g, *_: (0, 0, 0, 0)),
        ],
        out_specs=pl.BlockSpec((sector_count, width, width), lambda g, *_: (0, 0, 0)),
    )
    return pl.pallas_call(
        receiver_kernel,
        grid_spec=grid_spec,
        out_shape=jax.ShapeDtypeStruct((sector_count, width, width), jnp.float32),
        compiler_params=pltpu.CompilerParams(vmem_limit_bytes=48 * 1024 * 1024),
    )(labels, incoming, right_env)


def on_device(psi, left_env, right_env, target):
    item_of_slot, labels = slot_tables(target)
    labels_in = lax.all_to_all(labels, "sector", split_axis=0, concat_axis=0, tiled=True)
    outgoing = send_blocks(item_of_slot, labels, left_env, psi)
    incoming = lax.all_to_all(outgoing, "sector", split_axis=0, concat_axis=0, tiled=True)
    partial_value = receive_blocks(labels_in, incoming, right_env)
    term_count = lax.axis_size("term")
    sector_count, width, unused = partial_value.shape
    rows = width // term_count
    pieces = partial_value.reshape(sector_count, term_count, rows, width).transpose(1, 0, 2, 3)
    gathered = lax.all_to_all(pieces, "term", split_axis=0, concat_axis=0, tiled=True)
    return jnp.sum(gathered, axis=0)


def solution(mesh):
    in_specs = (
        P("sector", None, None),
        P("term", "sector", None, None),
        P("term", "sector", None, None),
        P("term", "sector"),
    )
    out_specs = P("sector", "term", None)
    return jax.shard_map(
        on_device, mesh=mesh, in_specs=in_specs, out_specs=out_specs, check_vma=False
    )
```

```python
import jax
import jax.numpy as jnp
from jax import lax
from jax.experimental import pallas as pl
from jax.experimental.pallas import tpu as pltpu
from jax.sharding import PartitionSpec as P

CAP = 4
GROUP = 8


def split_dot(a, b):
    a_hi = a.astype(jnp.bfloat16)
    a_lo = (a - a_hi.astype(jnp.float32)).astype(jnp.bfloat16)
    b_hi = b.astype(jnp.bfloat16)
    b_lo = (b - b_hi.astype(jnp.float32)).astype(jnp.bfloat16)

    def part(x, y):
        return jnp.dot(x, y, preferred_element_type=jnp.float32)

    return part(a_hi, b_hi) + (part(a_hi, b_lo) + part(a_lo, b_hi))


def slot_tables(target_part):
    term_count, sector_count = target_part.shape
    item_count = term_count * sector_count
    slot_count = lax.axis_size("sector") * CAP
    flat_target = target_part.reshape(item_count)
    owner_dev = flat_target // sector_count
    local_target = flat_target % sector_count
    item_index = jnp.arange(item_count, dtype=jnp.int32)
    term_index = item_index // sector_count
    earlier = (owner_dev[:, None] == owner_dev[None, :]) & (
        item_index[None, :] < item_index[:, None]
    )
    rank_slot = jnp.sum(earlier.astype(jnp.int32), axis=1)
    slot_index = owner_dev * CAP + rank_slot
    match = slot_index[None, :] == jnp.arange(slot_count, dtype=jnp.int32)[:, None]
    occupied = jnp.any(match, axis=1)
    item_of_slot = jnp.sum(jnp.where(match, item_index[None, :], 0), axis=1)
    label_of_item = term_index * sector_count + local_target + 1
    labels = jnp.where(occupied, label_of_item[item_of_slot], 0).astype(jnp.int32)
    return item_of_slot.astype(jnp.int32), labels


def sender_kernel(item_ref, label_ref, left_ref, psi_ref, out_ref):
    sector_count = psi_ref.shape[0]
    step = pl.program_id(0)
    for j in range(GROUP):
        slot = step * GROUP + j
        item = item_ref[slot]
        term = item // sector_count
        source = item % sector_count

        @pl.when(label_ref[slot] > 0)
        def _():
            out_ref[j] = split_dot(left_ref[term, source], psi_ref[source])

        @pl.when(label_ref[slot] == 0)
        def _():
            out_ref[j] = jnp.zeros(out_ref.shape[1:], jnp.float32)


def send_blocks(item_of_slot, labels, left_env, psi):
    slot_count = item_of_slot.shape[0]
    width = psi.shape[-1]
    grid_spec = pltpu.PrefetchScalarGridSpec(
        num_scalar_prefetch=2,
        grid=(slot_count // GROUP,),
        in_specs=[
            pl.BlockSpec(left_env.shape, lambda g, *_: (0, 0, 0, 0)),
            pl.BlockSpec(psi.shape, lambda g, *_: (0, 0, 0)),
        ],
        out_specs=pl.BlockSpec((GROUP, width, width), lambda g, *_: (g, 0, 0)),
    )
    return pl.pallas_call(
        sender_kernel,
        grid_spec=grid_spec,
        out_shape=jax.ShapeDtypeStruct((slot_count, width, width), jnp.float32),
        compiler_params=pltpu.CompilerParams(vmem_limit_bytes=48 * 1024 * 1024),
    )(item_of_slot, labels, left_env, psi)


def receiver_kernel(label_ref, incoming_ref, right_ref, out_ref):
    sector_count = out_ref.shape[0]
    step = pl.program_id(0)

    @pl.when(step == 0)
    def _():
        out_ref[...] = jnp.zeros(out_ref.shape, jnp.float32)

    for j in range(GROUP):
        label = label_ref[step * GROUP + j]

        @pl.when(label > 0)
        def _():
            pair = label - 1
            term = pair // sector_count
            tgt = pair % sector_count
            out_ref[tgt] += split_dot(incoming_ref[j], right_ref[term, tgt])


def receive_blocks(labels, incoming, right_env):
    slot_count = labels.shape[0]
    sector_count = right_env.shape[1]
    width = right_env.shape[-1]
    grid_spec = pltpu.PrefetchScalarGridSpec(
        num_scalar_prefetch=1,
        grid=(slot_count // GROUP,),
        in_specs=[
            pl.BlockSpec((GROUP, width, width), lambda g, *_: (g, 0, 0)),
            pl.BlockSpec(right_env.shape, lambda g, *_: (0, 0, 0, 0)),
        ],
        out_specs=pl.BlockSpec((sector_count, width, width), lambda g, *_: (0, 0, 0)),
    )
    return pl.pallas_call(
        receiver_kernel,
        grid_spec=grid_spec,
        out_shape=jax.ShapeDtypeStruct((sector_count, width, width), jnp.float32),
        compiler_params=pltpu.CompilerParams(vmem_limit_bytes=48 * 1024 * 1024),
    )(labels, incoming, right_env)


def on_device(psi, left_env, right_env, target):
    item_of_slot, labels = slot_tables(target)
    labels_in = lax.all_to_all(labels, "sector", split_axis=0, concat_axis=0, tiled=True)
    outgoing = send_blocks(item_of_slot, labels, left_env, psi)
    incoming = lax.all_to_all(outgoing, "sector", split_axis=0, concat_axis=0, tiled=True)
    partial_value = receive_blocks(labels_in, incoming, right_env)
    term_count = lax.axis_size("term")
    sector_count, width, unused = partial_value.shape
    rows = width // term_count
    pieces = partial_value.reshape(sector_count, term_count, rows, width).transpose(1, 0, 2, 3)
    gathered = lax.all_to_all(pieces, "term", split_axis=0, concat_axis=0, tiled=True)
    return jnp.sum(gathered, axis=0)


def solution(mesh):
    in_specs = (
        P("sector", None, None),
        P("term", "sector", None, None),
        P("term", "sector", None, None),
        P("term", "sector"),
    )
    out_specs = P("sector", "term", None)
    return jax.shard_map(
        on_device, mesh=mesh, in_specs=in_specs, out_specs=out_specs, check_vma=False
    )
```

```python
import functools

import jax
import jax.numpy as jnp
from jax import lax
from jax.experimental import pallas as pl
from jax.experimental.pallas import tpu as pltpu
from jax.sharding import PartitionSpec as P

CAP = 4
GROUP = 16
SPLIT = 2


def split_dot(a, b):
    a_hi = a.astype(jnp.bfloat16)
    a_lo = (a - a_hi.astype(jnp.float32)).astype(jnp.bfloat16)
    b_hi = b.astype(jnp.bfloat16)
    b_lo = (b - b_hi.astype(jnp.float32)).astype(jnp.bfloat16)

    def part(x, y):
        return jnp.dot(x, y, preferred_element_type=jnp.float32)

    return part(a_hi, b_hi) + (part(a_hi, b_lo) + part(a_lo, b_hi))


def slot_tables(target_part):
    term_count, sector_count = target_part.shape
    item_count = term_count * sector_count
    slot_count = lax.axis_size("sector") * CAP
    flat_target = target_part.reshape(item_count)
    owner_dev = flat_target // sector_count
    local_target = flat_target % sector_count
    item_index = jnp.arange(item_count, dtype=jnp.int32)
    term_index = item_index // sector_count
    earlier = (owner_dev[:, None] == owner_dev[None, :]) & (
        item_index[None, :] < item_index[:, None]
    )
    rank_slot = jnp.sum(earlier.astype(jnp.int32), axis=1)
    slot_index = owner_dev * CAP + rank_slot
    match = slot_index[None, :] == jnp.arange(slot_count, dtype=jnp.int32)[:, None]
    occupied = jnp.any(match, axis=1)
    item_of_slot = jnp.sum(jnp.where(match, item_index[None, :], 0), axis=1)
    label_of_item = term_index * sector_count + local_target + 1
    labels = jnp.where(occupied, label_of_item[item_of_slot], 0).astype(jnp.int32)
    return item_of_slot.astype(jnp.int32), labels


def sender_kernel(item_ref, label_ref, left_ref, psi_ref, *out_refs, term_count):
    sector_count = psi_ref.shape[0]
    width = psi_ref.shape[-1]
    band = width // term_count
    piece = band // SPLIT
    step = pl.program_id(0)
    for j in range(GROUP):
        slot = step * GROUP + j
        item = item_ref[slot]
        term = item // sector_count
        source = item % sector_count
        value = split_dot(left_ref[term, source], psi_ref[source])
        value = jnp.where(label_ref[slot] > 0, value, 0.0)
        for h, out_ref in enumerate(out_refs):
            for i in range(term_count):
                out_ref[j, pl.ds(i * piece, piece), :] = value[
                    i * band + h * piece:i * band + (h + 1) * piece, :
                ]


def send_blocks(item_of_slot, labels, left_env, psi, term_count):
    slot_count = item_of_slot.shape[0]
    width = psi.shape[-1]
    half = width // SPLIT
    grid_spec = pltpu.PrefetchScalarGridSpec(
        num_scalar_prefetch=2,
        grid=(slot_count // GROUP,),
        in_specs=[
            pl.BlockSpec(left_env.shape, lambda g, *_: (0, 0, 0, 0)),
            pl.BlockSpec(psi.shape, lambda g, *_: (0, 0, 0)),
        ],
        out_specs=[
            pl.BlockSpec((GROUP, half, width), lambda g, *_: (g, 0, 0)) for _ in range(SPLIT)
        ],
    )
    return pl.pallas_call(
        functools.partial(sender_kernel, term_count=term_count),
        grid_spec=grid_spec,
        out_shape=[
            jax.ShapeDtypeStruct((slot_count, half, width), jnp.float32) for _ in range(SPLIT)
        ],
        compiler_params=pltpu.CompilerParams(vmem_limit_bytes=48 * 1024 * 1024),
    )(item_of_slot, labels, left_env, psi)


def receiver_kernel(label_ref, incoming_ref, right_ref, out_ref):
    sector_count = out_ref.shape[0]
    step = pl.program_id(0)

    @pl.when(step == 0)
    def _():
        out_ref[...] = jnp.zeros(out_ref.shape, jnp.float32)

    targets = []
    values = []
    for j in range(GROUP):
        pair = jnp.maximum(label_ref[step * GROUP + j] - 1, 0)
        term = pair // sector_count
        tgt = pair % sector_count
        targets.append(tgt)
        values.append(split_dot(incoming_ref[j], right_ref[term, tgt]))
    for tgt, value in zip(targets, values):
        out_ref[tgt] += value


def receive_blocks(labels, incoming, right_env):
    slot_count = labels.shape[0]
    sector_count = right_env.shape[1]
    rows, width = incoming.shape[1:]
    grid_spec = pltpu.PrefetchScalarGridSpec(
        num_scalar_prefetch=1,
        grid=(slot_count // GROUP,),
        in_specs=[
            pl.BlockSpec((GROUP, rows, width), lambda g, *_: (g, 0, 0)),
            pl.BlockSpec(right_env.shape, lambda g, *_: (0, 0, 0, 0)),
        ],
        out_specs=pl.BlockSpec((sector_count, rows, width), lambda g, *_: (0, 0, 0)),
    )
    return pl.pallas_call(
        receiver_kernel,
        grid_spec=grid_spec,
        out_shape=jax.ShapeDtypeStruct((sector_count, rows, width), jnp.float32),
        compiler_params=pltpu.CompilerParams(vmem_limit_bytes=48 * 1024 * 1024),
    )(labels, incoming, right_env)


def on_device(psi, left_env, right_env, target):
    term_count = lax.axis_size("term")
    item_of_slot, labels = slot_tables(target)
    labels_in = lax.all_to_all(labels, "sector", split_axis=0, concat_axis=0, tiled=True)
    outgoing = send_blocks(item_of_slot, labels, left_env, psi, term_count)
    results = []
    for piece_out in outgoing:
        incoming = lax.all_to_all(piece_out, "sector", split_axis=0, concat_axis=0, tiled=True)
        partial_value = receive_blocks(labels_in, incoming, right_env)
        sector_count, rows, width = partial_value.shape
        pieces = partial_value.reshape(sector_count, term_count, rows // term_count, width)
        pieces = pieces.transpose(1, 0, 2, 3)
        gathered = lax.all_to_all(pieces, "term", split_axis=0, concat_axis=0, tiled=True)
        results.append(jnp.sum(gathered, axis=0))
    return jnp.concatenate(results, axis=1)


def solution(mesh):
    in_specs = (
        P("sector", None, None),
        P("term", "sector", None, None),
        P("term", "sector", None, None),
        P("term", "sector"),
    )
    out_specs = P("sector", "term", None)
    return jax.shard_map(
        on_device, mesh=mesh, in_specs=in_specs, out_specs=out_specs, check_vma=False
    )
```

```python
import functools

import jax
import jax.numpy as jnp
from jax import lax
from jax.experimental import pallas as pl
from jax.experimental.pallas import tpu as pltpu
from jax.sharding import PartitionSpec as P

CAP = 4
GROUP = 16
SPLIT = 2


def split_dot(a, b):
    a_hi = a.astype(jnp.bfloat16)
    a_lo = (a - a_hi.astype(jnp.float32)).astype(jnp.bfloat16)
    b_hi = b.astype(jnp.bfloat16)
    b_lo = (b - b_hi.astype(jnp.float32)).astype(jnp.bfloat16)

    def part(x, y):
        return jnp.dot(x, y, preferred_element_type=jnp.float32)

    return part(a_hi, b_hi) + (part(a_hi, b_lo) + part(a_lo, b_hi))


def slot_tables(target_part):
    term_count, sector_count = target_part.shape
    item_count = term_count * sector_count
    slot_count = lax.axis_size("sector") * CAP
    flat_target = target_part.reshape(item_count)
    owner_dev = flat_target // sector_count
    local_target = flat_target % sector_count
    item_index = jnp.arange(item_count, dtype=jnp.int32)
    term_index = item_index // sector_count
    earlier = (owner_dev[:, None] == owner_dev[None, :]) & (
        item_index[None, :] < item_index[:, None]
    )
    rank_slot = jnp.sum(earlier.astype(jnp.int32), axis=1)
    slot_index = owner_dev * CAP + rank_slot
    match = slot_index[None, :] == jnp.arange(slot_count, dtype=jnp.int32)[:, None]
    occupied = jnp.any(match, axis=1)
    item_of_slot = jnp.sum(jnp.where(match, item_index[None, :], 0), axis=1)
    label_of_item = term_index * sector_count + local_target + 1
    labels = jnp.where(occupied, label_of_item[item_of_slot], 0).astype(jnp.int32)
    return item_of_slot.astype(jnp.int32), labels


def sender_kernel(item_ref, label_ref, left_ref, psi_ref, out_ref, *, term_count, half):
    sector_count = psi_ref.shape[0]
    width = psi_ref.shape[-1]
    band = width // term_count
    piece = band // SPLIT
    step = pl.program_id(0)
    for j in range(GROUP):
        slot = step * GROUP + j
        item = item_ref[slot]
        term = item // sector_count
        source = item % sector_count
        rows = jnp.concatenate(
            [left_ref[term, source, pl.ds(i * band + half * piece, piece), :] for i in range(term_count)],
            axis=0,
        )
        value = split_dot(rows, psi_ref[source])
        out_ref[j] = jnp.where(label_ref[slot] > 0, value, 0.0)


def send_blocks(item_of_slot, labels, left_env, psi, term_count, half):
    slot_count = item_of_slot.shape[0]
    width = psi.shape[-1]
    rows = width // SPLIT
    grid_spec = pltpu.PrefetchScalarGridSpec(
        num_scalar_prefetch=2,
        grid=(slot_count // GROUP,),
        in_specs=[
            pl.BlockSpec(left_env.shape, lambda g, *_: (0, 0, 0, 0)),
            pl.BlockSpec(psi.shape, lambda g, *_: (0, 0, 0)),
        ],
        out_specs=pl.BlockSpec((GROUP, rows, width), lambda g, *_: (g, 0, 0)),
    )
    return pl.pallas_call(
        functools.partial(sender_kernel, term_count=term_count, half=half),
        grid_spec=grid_spec,
        out_shape=jax.ShapeDtypeStruct((slot_count, rows, width), jnp.float32),
        compiler_params=pltpu.CompilerParams(vmem_limit_bytes=48 * 1024 * 1024),
    )(item_of_slot, labels, left_env, psi)


def receiver_kernel(label_ref, incoming_ref, right_ref, out_ref):
    sector_count = out_ref.shape[0]
    step = pl.program_id(0)

    @pl.when(step == 0)
    def _():
        out_ref[...] = jnp.zeros(out_ref.shape, jnp.float32)

    targets = []
    values = []
    for j in range(GROUP):
        pair = jnp.maximum(label_ref[step * GROUP + j] - 1, 0)
        term = pair // sector_count
        tgt = pair % sector_count
        targets.append(tgt)
        values.append(split_dot(incoming_ref[j], right_ref[term, tgt]))
    for tgt, value in zip(targets, values):
        out_ref[tgt] += value


def receive_blocks(labels, incoming, right_env):
    slot_count = labels.shape[0]
    sector_count = right_env.shape[1]
    rows, width = incoming.shape[1:]
    grid_spec = pltpu.PrefetchScalarGridSpec(
        num_scalar_prefetch=1,
        grid=(slot_count // GROUP,),
        in_specs=[
            pl.BlockSpec((GROUP, rows, width), lambda g, *_: (g, 0, 0)),
            pl.BlockSpec(right_env.shape, lambda g, *_: (0, 0, 0, 0)),
        ],
        out_specs=pl.BlockSpec((sector_count, rows, width), lambda g, *_: (0, 0, 0)),
    )
    return pl.pallas_call(
        receiver_kernel,
        grid_spec=grid_spec,
        out_shape=jax.ShapeDtypeStruct((sector_count, rows, width), jnp.float32),
        compiler_params=pltpu.CompilerParams(vmem_limit_bytes=48 * 1024 * 1024),
    )(labels, incoming, right_env)


def incoming_labels(target):
    term_count, sector_count = target.shape
    device_count = lax.axis_size("sector")
    everyone = lax.all_gather(target, "sector", axis=1, tiled=True)
    everyone = everyone.reshape(term_count, device_count, sector_count).transpose(1, 0, 2)
    unused, labels_all = jax.vmap(slot_tables)(everyone)
    mine = lax.axis_index("sector")
    labels_in = lax.dynamic_slice_in_dim(labels_all, mine * CAP, CAP, axis=1)
    return labels_in.reshape(device_count * CAP)


def on_device(psi, left_env, right_env, target):
    term_count = lax.axis_size("term")
    item_of_slot, labels = slot_tables(target)
    labels_in = incoming_labels(target)
    results = []
    for half in range(SPLIT):
        piece_out = send_blocks(item_of_slot, labels, left_env, psi, term_count, half)
        incoming = lax.all_to_all(piece_out, "sector", split_axis=0, concat_axis=0, tiled=True)
        partial_value = receive_blocks(labels_in, incoming, right_env)
        sector_count, rows, width = partial_value.shape
        pieces = partial_value.reshape(sector_count, term_count, rows // term_count, width)
        pieces = pieces.transpose(1, 0, 2, 3)
        gathered = lax.all_to_all(pieces, "term", split_axis=0, concat_axis=0, tiled=True)
        results.append(jnp.sum(gathered, axis=0))
    return jnp.concatenate(results, axis=1)


def solution(mesh):
    in_specs = (
        P("sector", None, None),
        P("term", "sector", None, None),
        P("term", "sector", None, None),
        P("term", "sector"),
    )
    out_specs = P("sector", "term", None)
    return jax.shard_map(
        on_device, mesh=mesh, in_specs=in_specs, out_specs=out_specs, check_vma=False
    )
```

```python
import functools

import jax
import jax.numpy as jnp
from jax import lax
from jax.experimental import pallas as pl
from jax.experimental.pallas import tpu as pltpu
from jax.sharding import PartitionSpec as P

CAP = 4
GROUP = 16
SPLIT = 2


def split_dot(a, b):
    a_hi = a.astype(jnp.bfloat16)
    a_lo = (a - a_hi.astype(jnp.float32)).astype(jnp.bfloat16)
    b_hi = b.astype(jnp.bfloat16)
    b_lo = (b - b_hi.astype(jnp.float32)).astype(jnp.bfloat16)

    def part(x, y):
        return jnp.dot(x, y, preferred_element_type=jnp.float32)

    return part(a_hi, b_hi) + (part(a_hi, b_lo) + part(a_lo, b_hi))


def slot_tables(target_part):
    term_count, sector_count = target_part.shape
    item_count = term_count * sector_count
    slot_count = lax.axis_size("sector") * CAP
    flat_target = target_part.reshape(item_count)
    owner_dev = flat_target // sector_count
    local_target = flat_target % sector_count
    item_index = jnp.arange(item_count, dtype=jnp.int32)
    term_index = item_index // sector_count
    earlier = (owner_dev[:, None] == owner_dev[None, :]) & (
        item_index[None, :] < item_index[:, None]
    )
    rank_slot = jnp.sum(earlier.astype(jnp.int32), axis=1)
    slot_index = owner_dev * CAP + rank_slot
    match = slot_index[None, :] == jnp.arange(slot_count, dtype=jnp.int32)[:, None]
    occupied = jnp.any(match, axis=1)
    item_of_slot = jnp.sum(jnp.where(match, item_index[None, :], 0), axis=1)
    label_of_item = term_index * sector_count + local_target + 1
    labels = jnp.where(occupied, label_of_item[item_of_slot], 0).astype(jnp.int32)
    return item_of_slot.astype(jnp.int32), labels


def sender_kernel(item_ref, label_ref, left_ref, psi_ref, out_ref, *, term_count, half):
    sector_count = psi_ref.shape[0]
    width = psi_ref.shape[-1]
    band = width // term_count
    piece = band // SPLIT
    step = pl.program_id(0)
    for j in range(GROUP):
        slot = step * GROUP + j
        item = item_ref[slot]
        term = item // sector_count
        source = item % sector_count
        rows = jnp.concatenate(
            [left_ref[term, source, pl.ds(i * band + half * piece, piece), :] for i in range(term_count)],
            axis=0,
        )
        value = split_dot(rows, psi_ref[source])
        out_ref[j] = jnp.where(label_ref[slot] > 0, value, 0.0)


def send_blocks(item_of_slot, labels, left_env, psi, term_count, half):
    slot_count = item_of_slot.shape[0]
    width = psi.shape[-1]
    rows = width // SPLIT
    grid_spec = pltpu.PrefetchScalarGridSpec(
        num_scalar_prefetch=2,
        grid=(slot_count // GROUP,),
        in_specs=[
            pl.BlockSpec(left_env.shape, lambda g, *_: (0, 0, 0, 0)),
            pl.BlockSpec(psi.shape, lambda g, *_: (0, 0, 0)),
        ],
        out_specs=pl.BlockSpec((GROUP, rows, width), lambda g, *_: (g, 0, 0)),
    )
    return pl.pallas_call(
        functools.partial(sender_kernel, term_count=term_count, half=half),
        grid_spec=grid_spec,
        out_shape=jax.ShapeDtypeStruct((slot_count, rows, width), jnp.float32),
        compiler_params=pltpu.CompilerParams(vmem_limit_bytes=48 * 1024 * 1024),
    )(item_of_slot, labels, left_env, psi)


def receiver_kernel(label_ref, incoming_ref, right_ref, out_ref):
    sector_count = out_ref.shape[0]
    step = pl.program_id(0)

    @pl.when(step == 0)
    def _():
        out_ref[...] = jnp.zeros(out_ref.shape, jnp.float32)

    targets = []
    values = []
    for j in range(GROUP):
        pair = jnp.maximum(label_ref[step * GROUP + j] - 1, 0)
        term = pair // sector_count
        tgt = pair % sector_count
        targets.append(tgt)
        values.append(split_dot(incoming_ref[j], right_ref[term, tgt]))
    for tgt, value in zip(targets, values):
        out_ref[tgt] += value


def receive_blocks(labels, incoming, right_env):
    slot_count = labels.shape[0]
    sector_count = right_env.shape[1]
    rows, width = incoming.shape[1:]
    grid_spec = pltpu.PrefetchScalarGridSpec(
        num_scalar_prefetch=1,
        grid=(slot_count // GROUP,),
        in_specs=[
            pl.BlockSpec((GROUP, rows, width), lambda g, *_: (g, 0, 0)),
            pl.BlockSpec(right_env.shape, lambda g, *_: (0, 0, 0, 0)),
        ],
        out_specs=pl.BlockSpec((sector_count, rows, width), lambda g, *_: (0, 0, 0)),
    )
    return pl.pallas_call(
        receiver_kernel,
        grid_spec=grid_spec,
        out_shape=jax.ShapeDtypeStruct((sector_count, rows, width), jnp.float32),
        compiler_params=pltpu.CompilerParams(vmem_limit_bytes=48 * 1024 * 1024),
    )(labels, incoming, right_env)


def term_exchange(partial_value, term_count):
    sector_count, rows, width = partial_value.shape
    pieces = partial_value.reshape(sector_count, term_count, rows // term_count, width)
    mine = lax.axis_index("term")
    total = lax.dynamic_index_in_dim(pieces, mine, axis=1, keepdims=False)
    for shift in range(1, term_count):
        sent = lax.dynamic_index_in_dim(pieces, (mine + shift) % term_count, axis=1, keepdims=False)
        pairs = [(dev, (dev + shift) % term_count) for dev in range(term_count)]
        total = total + lax.ppermute(sent, "term", pairs)
    return total


def on_device(psi, left_env, right_env, target):
    term_count = lax.axis_size("term")
    item_of_slot, labels = slot_tables(target)
    labels_in = lax.all_to_all(labels, "sector", split_axis=0, concat_axis=0, tiled=True)
    results = []
    for half in range(SPLIT):
        piece_out = send_blocks(item_of_slot, labels, left_env, psi, term_count, half)
        incoming = lax.all_to_all(piece_out, "sector", split_axis=0, concat_axis=0, tiled=True)
        partial_value = receive_blocks(labels_in, incoming, right_env)
        results.append(term_exchange(partial_value, term_count))
    return jnp.concatenate(results, axis=1)


def solution(mesh):
    in_specs = (
        P("sector", None, None),
        P("term", "sector", None, None),
        P("term", "sector", None, None),
        P("term", "sector"),
    )
    out_specs = P("sector", "term", None)
    return jax.shard_map(
        on_device, mesh=mesh, in_specs=in_specs, out_specs=out_specs, check_vma=False
    )
```

```python
import functools

import jax
import jax.numpy as jnp
from jax import lax
from jax.experimental import pallas as pl
from jax.experimental.pallas import tpu as pltpu
from jax.sharding import PartitionSpec as P

CAP = 4
GROUP = 16
SPLIT = 2


def split_dot(a, b):
    rows = a.shape[0]
    a_hi = a.astype(jnp.bfloat16)
    a_lo = (a - a_hi.astype(jnp.float32)).astype(jnp.bfloat16)
    b_hi = b.astype(jnp.bfloat16)
    b_lo = (b - b_hi.astype(jnp.float32)).astype(jnp.bfloat16)
    both = jnp.dot(
        jnp.concatenate([a_hi, a_lo], axis=0), b_hi, preferred_element_type=jnp.float32
    )
    cross = jnp.dot(a_hi, b_lo, preferred_element_type=jnp.float32)
    return both[:rows] + (cross + both[rows:])


def slot_tables(target_part):
    term_count, sector_count = target_part.shape
    item_count = term_count * sector_count
    slot_count = lax.axis_size("sector") * CAP
    flat_target = target_part.reshape(item_count)
    owner_dev = flat_target // sector_count
    local_target = flat_target % sector_count
    item_index = jnp.arange(item_count, dtype=jnp.int32)
    term_index = item_index // sector_count
    earlier = (owner_dev[:, None] == owner_dev[None, :]) & (
        item_index[None, :] < item_index[:, None]
    )
    rank_slot = jnp.sum(earlier.astype(jnp.int32), axis=1)
    slot_index = owner_dev * CAP + rank_slot
    match = slot_index[None, :] == jnp.arange(slot_count, dtype=jnp.int32)[:, None]
    occupied = jnp.any(match, axis=1)
    item_of_slot = jnp.sum(jnp.where(match, item_index[None, :], 0), axis=1)
    label_of_item = term_index * sector_count + local_target + 1
    labels = jnp.where(occupied, label_of_item[item_of_slot], 0).astype(jnp.int32)
    return item_of_slot.astype(jnp.int32), labels


def sender_kernel(item_ref, label_ref, left_ref, psi_ref, out_ref, *, term_count, half):
    sector_count = psi_ref.shape[0]
    width = psi_ref.shape[-1]
    band = width // term_count
    piece = band // SPLIT
    step = pl.program_id(0)
    for j in range(GROUP):
        slot = step * GROUP + j
        item = item_ref[slot]
        term = item // sector_count
        source = item % sector_count
        rows = jnp.concatenate(
            [left_ref[term, source, pl.ds(i * band + half * piece, piece), :] for i in range(term_count)],
            axis=0,
        )
        value = split_dot(rows, psi_ref[source])
        out_ref[j] = jnp.where(label_ref[slot] > 0, value, 0.0)


def send_blocks(item_of_slot, labels, left_env, psi, term_count, half):
    slot_count = item_of_slot.shape[0]
    width = psi.shape[-1]
    rows = width // SPLIT
    grid_spec = pltpu.PrefetchScalarGridSpec(
        num_scalar_prefetch=2,
        grid=(slot_count // GROUP,),
        in_specs=[
            pl.BlockSpec(left_env.shape, lambda g, *_: (0, 0, 0, 0)),
            pl.BlockSpec(psi.shape, lambda g, *_: (0, 0, 0)),
        ],
        out_specs=pl.BlockSpec((GROUP, rows, width), lambda g, *_: (g, 0, 0)),
    )
    return pl.pallas_call(
        functools.partial(sender_kernel, term_count=term_count, half=half),
        grid_spec=grid_spec,
        out_shape=jax.ShapeDtypeStruct((slot_count, rows, width), jnp.float32),
        compiler_params=pltpu.CompilerParams(vmem_limit_bytes=48 * 1024 * 1024),
    )(item_of_slot, labels, left_env, psi)


def receiver_kernel(label_ref, incoming_ref, right_ref, out_ref):
    sector_count = out_ref.shape[0]
    step = pl.program_id(0)

    @pl.when(step == 0)
    def _():
        out_ref[...] = jnp.zeros(out_ref.shape, jnp.float32)

    targets = []
    values = []
    for j in range(GROUP):
        pair = jnp.maximum(label_ref[step * GROUP + j] - 1, 0)
        term = pair // sector_count
        tgt = pair % sector_count
        targets.append(tgt)
        values.append(split_dot(incoming_ref[j], right_ref[term, tgt]))
    for tgt, value in zip(targets, values):
        out_ref[tgt] += value


def receive_blocks(labels, incoming, right_env):
    slot_count = labels.shape[0]
    sector_count = right_env.shape[1]
    rows, width = incoming.shape[1:]
    grid_spec = pltpu.PrefetchScalarGridSpec(
        num_scalar_prefetch=1,
        grid=(slot_count // GROUP,),
        in_specs=[
            pl.BlockSpec((GROUP, rows, width), lambda g, *_: (g, 0, 0)),
            pl.BlockSpec(right_env.shape, lambda g, *_: (0, 0, 0, 0)),
        ],
        out_specs=pl.BlockSpec((sector_count, rows, width), lambda g, *_: (0, 0, 0)),
    )
    return pl.pallas_call(
        receiver_kernel,
        grid_spec=grid_spec,
        out_shape=jax.ShapeDtypeStruct((sector_count, rows, width), jnp.float32),
        compiler_params=pltpu.CompilerParams(vmem_limit_bytes=48 * 1024 * 1024),
    )(labels, incoming, right_env)


def term_exchange(partial_value, term_count):
    sector_count, rows, width = partial_value.shape
    pieces = partial_value.reshape(sector_count, term_count, rows // term_count, width)
    mine = lax.axis_index("term")
    total = lax.dynamic_index_in_dim(pieces, mine, axis=1, keepdims=False)
    for shift in range(1, term_count):
        sent = lax.dynamic_index_in_dim(pieces, (mine + shift) % term_count, axis=1, keepdims=False)
        pairs = [(dev, (dev + shift) % term_count) for dev in range(term_count)]
        total = total + lax.ppermute(sent, "term", pairs)
    return total


def term_all_to_all(partial_value, term_count):
    sector_count, rows, width = partial_value.shape
    pieces = partial_value.reshape(sector_count, term_count, rows // term_count, width)
    pieces = pieces.transpose(1, 0, 2, 3)
    gathered = lax.all_to_all(pieces, "term", split_axis=0, concat_axis=0, tiled=True)
    return jnp.sum(gathered, axis=0)


def on_device(psi, left_env, right_env, target):
    term_count = lax.axis_size("term")
    item_of_slot, labels = slot_tables(target)
    labels_in = lax.all_to_all(labels, "sector", split_axis=0, concat_axis=0, tiled=True)
    results = []
    for half in range(SPLIT):
        piece_out = send_blocks(item_of_slot, labels, left_env, psi, term_count, half)
        incoming = lax.all_to_all(piece_out, "sector", split_axis=0, concat_axis=0, tiled=True)
        partial_value = receive_blocks(labels_in, incoming, right_env)
        if half + 1 < SPLIT:
            results.append(term_exchange(partial_value, term_count))
        else:
            results.append(term_all_to_all(partial_value, term_count))
    return jnp.concatenate(results, axis=1)


def solution(mesh):
    in_specs = (
        P("sector", None, None),
        P("term", "sector", None, None),
        P("term", "sector", None, None),
        P("term", "sector"),
    )
    out_specs = P("sector", "term", None)
    return jax.shard_map(
        on_device, mesh=mesh, in_specs=in_specs, out_specs=out_specs, check_vma=False
    )
```

```python
import functools

import jax
import jax.numpy as jnp
from jax import lax
from jax.experimental import pallas as pl
from jax.experimental.pallas import tpu as pltpu
from jax.sharding import PartitionSpec as P

CAP = 4
GROUP = 8
SENDER_STEPS = 4
SPLIT = 2


def split_dot(a, b):
    rows = a.shape[0]
    a_hi = a.astype(jnp.bfloat16)
    a_lo = (a - a_hi.astype(jnp.float32)).astype(jnp.bfloat16)
    b_hi = b.astype(jnp.bfloat16)
    b_lo = (b - b_hi.astype(jnp.float32)).astype(jnp.bfloat16)
    both = jnp.dot(
        jnp.concatenate([a_hi, a_lo], axis=0), b_hi, preferred_element_type=jnp.float32
    )
    cross = jnp.dot(a_hi, b_lo, preferred_element_type=jnp.float32)
    return both[:rows] + (cross + both[rows:])


def slot_tables(target_part):
    term_count, sector_count = target_part.shape
    item_count = term_count * sector_count
    slot_count = lax.axis_size("sector") * CAP
    flat_target = target_part.reshape(item_count)
    owner_dev = flat_target // sector_count
    local_target = flat_target % sector_count
    item_index = jnp.arange(item_count, dtype=jnp.int32)
    term_index = item_index // sector_count
    earlier = (owner_dev[:, None] == owner_dev[None, :]) & (
        item_index[None, :] < item_index[:, None]
    )
    rank_slot = jnp.sum(earlier.astype(jnp.int32), axis=1)
    slot_index = jnp.minimum(owner_dev * CAP + rank_slot, slot_count - 1).astype(jnp.int32)
    slot_range = jnp.arange(slot_count, dtype=jnp.int32)
    match = slot_index[None, :] == slot_range[:, None]
    occupied = jnp.any(match, axis=1)
    item_of_slot = jnp.sum(jnp.where(match, item_index[None, :], 0), axis=1)
    label_of_item = term_index * sector_count + local_target + 1
    labels = jnp.where(occupied, label_of_item[item_of_slot], 0).astype(jnp.int32)
    return slot_index, compact_order(~occupied), labels


def compact_order(flags):
    count = flags.shape[0]
    first = jnp.cumsum(flags.astype(jnp.int32)) - 1
    rest = jnp.sum(flags.astype(jnp.int32)) + jnp.cumsum((~flags).astype(jnp.int32)) - 1
    position = jnp.where(flags, first, rest)
    spots = jnp.arange(count, dtype=jnp.int32)
    chosen = position[None, :] == spots[:, None]
    return jnp.sum(jnp.where(chosen, spots[None, :], 0), axis=1).astype(jnp.int32)


def sender_kernel(slot_ref, empty_ref, left_ref, psi_ref, out_ref, *, term_count, half):
    terms, sector_count = left_ref.shape[:2]
    width = psi_ref.shape[-1]
    band = width // term_count
    piece = band // SPLIT
    step = pl.program_id(0)
    per_step = sector_count // SENDER_STEPS

    @pl.when(step == 0)
    def _():
        for k in range(out_ref.shape[0] - terms * sector_count):
            out_ref[empty_ref[k]] = jnp.zeros(out_ref.shape[1:], jnp.float32)

    for j in range(per_step):
        source = step * per_step + j
        rows = jnp.concatenate(
            [
                left_ref[w, source, pl.ds(i * band + half * piece, piece), :]
                for w in range(terms)
                for i in range(term_count)
            ],
            axis=0,
        )
        value = split_dot(rows, psi_ref[source])
        for w in range(terms):
            out_ref[slot_ref[w * sector_count + source]] = value[w * piece * term_count:(w + 1) * piece * term_count]


def send_blocks(slot_index, empty_slots, left_env, psi, term_count, half):
    slot_count = empty_slots.shape[0]
    width = psi.shape[-1]
    rows = width // SPLIT
    grid_spec = pltpu.PrefetchScalarGridSpec(
        num_scalar_prefetch=2,
        grid=(SENDER_STEPS,),
        in_specs=[
            pl.BlockSpec(left_env.shape, lambda g, *_: (0, 0, 0, 0)),
            pl.BlockSpec(psi.shape, lambda g, *_: (0, 0, 0)),
        ],
        out_specs=pl.BlockSpec((slot_count, rows, width), lambda g, *_: (0, 0, 0)),
    )
    return pl.pallas_call(
        functools.partial(sender_kernel, term_count=term_count, half=half),
        grid_spec=grid_spec,
        out_shape=jax.ShapeDtypeStruct((slot_count, rows, width), jnp.float32),
        compiler_params=pltpu.CompilerParams(vmem_limit_bytes=48 * 1024 * 1024),
    )(slot_index, empty_slots, left_env, psi)


def receiver_kernel(order_ref, count_ref, label_ref, incoming_ref, right_ref, out_ref):
    sector_count = out_ref.shape[0]
    out_ref[...] = jnp.zeros(out_ref.shape, jnp.float32)

    def body(g, carry):
        targets = []
        values = []
        for j in range(GROUP):
            slot = order_ref[g * GROUP + j]
            pair = jnp.maximum(label_ref[slot] - 1, 0)
            term = pair // sector_count
            tgt = pair % sector_count
            targets.append(tgt)
            values.append(split_dot(incoming_ref[slot], right_ref[term, tgt]))
        for tgt, value in zip(targets, values):
            out_ref[tgt] += value
        return carry

    lax.fori_loop(0, (count_ref[0] + GROUP - 1) // GROUP, body, 0)


def receive_blocks(labels, incoming, right_env):
    sector_count = right_env.shape[1]
    slot_count, rows, width = incoming.shape
    occupied = labels > 0
    order = compact_order(occupied)
    count = jnp.sum(occupied.astype(jnp.int32)).reshape(1)
    grid_spec = pltpu.PrefetchScalarGridSpec(
        num_scalar_prefetch=3,
        grid=(1,),
        in_specs=[
            pl.BlockSpec(incoming.shape, lambda g, *_: (0, 0, 0)),
            pl.BlockSpec(right_env.shape, lambda g, *_: (0, 0, 0, 0)),
        ],
        out_specs=pl.BlockSpec((sector_count, rows, width), lambda g, *_: (0, 0, 0)),
    )
    return pl.pallas_call(
        receiver_kernel,
        grid_spec=grid_spec,
        out_shape=jax.ShapeDtypeStruct((sector_count, rows, width), jnp.float32),
        compiler_params=pltpu.CompilerParams(vmem_limit_bytes=48 * 1024 * 1024),
    )(order, count, labels, incoming, right_env)


def term_exchange(partial_value, term_count):
    sector_count, rows, width = partial_value.shape
    pieces = partial_value.reshape(sector_count, term_count, rows // term_count, width)
    mine = lax.axis_index("term")
    total = lax.dynamic_index_in_dim(pieces, mine, axis=1, keepdims=False)
    for shift in range(1, term_count):
        sent = lax.dynamic_index_in_dim(pieces, (mine + shift) % term_count, axis=1, keepdims=False)
        pairs = [(dev, (dev + shift) % term_count) for dev in range(term_count)]
        total = total + lax.ppermute(sent, "term", pairs)
    return total


def on_device(psi, left_env, right_env, target):
    term_count = lax.axis_size("term")
    slot_index, empty_slots, labels = slot_tables(target)
    labels_in = lax.all_to_all(labels, "sector", split_axis=0, concat_axis=0, tiled=True)
    results = []
    for half in range(SPLIT):
        piece_out = send_blocks(slot_index, empty_slots, left_env, psi, term_count, half)
        incoming = lax.all_to_all(piece_out, "sector", split_axis=0, concat_axis=0, tiled=True)
        partial_value = receive_blocks(labels_in, incoming, right_env)
        results.append(term_exchange(partial_value, term_count))
    return jnp.concatenate(results, axis=1)


def solution(mesh):
    in_specs = (
        P("sector", None, None),
        P("term", "sector", None, None),
        P("term", "sector", None, None),
        P("term", "sector"),
    )
    out_specs = P("sector", "term", None)
    return jax.shard_map(
        on_device, mesh=mesh, in_specs=in_specs, out_specs=out_specs, check_vma=False
    )
```

```python
import functools

import jax
import jax.numpy as jnp
from jax import lax
from jax.experimental import pallas as pl
from jax.experimental.pallas import tpu as pltpu
from jax.sharding import PartitionSpec as P

CAP = 4
GROUP = 8
SENDER_STEPS = 4
SPLIT = 2


def split_dot(a, b):
    rows = a.shape[0]
    a_hi = a.astype(jnp.bfloat16)
    a_lo = (a - a_hi.astype(jnp.float32)).astype(jnp.bfloat16)
    b_hi = b.astype(jnp.bfloat16)
    b_lo = (b - b_hi.astype(jnp.float32)).astype(jnp.bfloat16)
    both = jnp.dot(
        jnp.concatenate([a_hi, a_lo], axis=0), b_hi, preferred_element_type=jnp.float32
    )
    cross = jnp.dot(a_hi, b_lo, preferred_element_type=jnp.float32)
    return both[:rows] + (cross + both[rows:])


def slot_tables(target_part):
    term_count, sector_count = target_part.shape
    item_count = term_count * sector_count
    slot_count = lax.axis_size("sector") * CAP
    flat_target = target_part.reshape(item_count)
    owner_dev = flat_target // sector_count
    local_target = flat_target % sector_count
    item_index = jnp.arange(item_count, dtype=jnp.int32)
    term_index = item_index // sector_count
    earlier = (owner_dev[:, None] == owner_dev[None, :]) & (
        item_index[None, :] < item_index[:, None]
    )
    rank_slot = jnp.sum(earlier.astype(jnp.int32), axis=1)
    slot_index = jnp.minimum(owner_dev * CAP + rank_slot, slot_count - 1).astype(jnp.int32)
    slot_range = jnp.arange(slot_count, dtype=jnp.int32)
    match = slot_index[None, :] == slot_range[:, None]
    occupied = jnp.any(match, axis=1)
    item_of_slot = jnp.sum(jnp.where(match, item_index[None, :], 0), axis=1)
    label_of_item = term_index * sector_count + local_target + 1
    labels = jnp.where(occupied, label_of_item[item_of_slot], 0).astype(jnp.int32)
    return slot_index, compact_order(~occupied), labels


def compact_order(flags):
    count = flags.shape[0]
    first = jnp.cumsum(flags.astype(jnp.int32)) - 1
    rest = jnp.sum(flags.astype(jnp.int32)) + jnp.cumsum((~flags).astype(jnp.int32)) - 1
    position = jnp.where(flags, first, rest)
    spots = jnp.arange(count, dtype=jnp.int32)
    chosen = position[None, :] == spots[:, None]
    return jnp.sum(jnp.where(chosen, spots[None, :], 0), axis=1).astype(jnp.int32)


def sender_kernel(slot_ref, empty_ref, left_ref, psi_ref, out_ref, *, term_count, half):
    terms, sector_count = left_ref.shape[:2]
    width = psi_ref.shape[-1]
    band = width // term_count
    piece = band // SPLIT
    step = pl.program_id(0)
    per_step = sector_count // SENDER_STEPS

    @pl.when(step == 0)
    def _():
        for k in range(out_ref.shape[0] - terms * sector_count):
            out_ref[empty_ref[k]] = jnp.zeros(out_ref.shape[1:], jnp.float32)

    for j in range(per_step):
        source = step * per_step + j
        rows = jnp.concatenate(
            [
                left_ref[w, source, pl.ds(i * band + half * piece, piece), :]
                for w in range(terms)
                for i in range(term_count)
            ],
            axis=0,
        )
        value = split_dot(rows, psi_ref[source])
        for w in range(terms):
            out_ref[slot_ref[w * sector_count + source]] = value[w * piece * term_count:(w + 1) * piece * term_count]


def send_blocks(slot_index, empty_slots, left_env, psi, term_count, half):
    slot_count = empty_slots.shape[0]
    width = psi.shape[-1]
    rows = width // SPLIT
    grid_spec = pltpu.PrefetchScalarGridSpec(
        num_scalar_prefetch=2,
        grid=(SENDER_STEPS,),
        in_specs=[
            pl.BlockSpec(left_env.shape, lambda g, *_: (0, 0, 0, 0)),
            pl.BlockSpec(psi.shape, lambda g, *_: (0, 0, 0)),
        ],
        out_specs=pl.BlockSpec((slot_count, rows, width), lambda g, *_: (0, 0, 0)),
    )
    return pl.pallas_call(
        functools.partial(sender_kernel, term_count=term_count, half=half),
        grid_spec=grid_spec,
        out_shape=jax.ShapeDtypeStruct((slot_count, rows, width), jnp.float32),
        compiler_params=pltpu.CompilerParams(vmem_limit_bytes=48 * 1024 * 1024),
    )(slot_index, empty_slots, left_env, psi)


def receiver_kernel(order_ref, count_ref, label_ref, incoming_ref, right_ref, out_ref):
    sector_count = out_ref.shape[0]
    out_ref[...] = jnp.zeros(out_ref.shape, jnp.float32)

    def body(g, carry):
        targets = []
        values = []
        for j in range(GROUP):
            slot = order_ref[g * GROUP + j]
            pair = jnp.maximum(label_ref[slot] - 1, 0)
            term = pair // sector_count
            tgt = pair % sector_count
            targets.append(tgt)
            values.append(split_dot(incoming_ref[slot], right_ref[term, tgt]))
        for tgt, value in zip(targets, values):
            out_ref[tgt] += value
        return carry

    lax.fori_loop(0, (count_ref[0] + GROUP - 1) // GROUP, body, 0)


def receive_blocks(labels, incoming, right_env):
    sector_count = right_env.shape[1]
    slot_count, rows, width = incoming.shape
    occupied = labels > 0
    order = compact_order(occupied)
    count = jnp.sum(occupied.astype(jnp.int32)).reshape(1)
    grid_spec = pltpu.PrefetchScalarGridSpec(
        num_scalar_prefetch=3,
        grid=(1,),
        in_specs=[
            pl.BlockSpec(incoming.shape, lambda g, *_: (0, 0, 0)),
            pl.BlockSpec(right_env.shape, lambda g, *_: (0, 0, 0, 0)),
        ],
        out_specs=pl.BlockSpec((sector_count, rows, width), lambda g, *_: (0, 0, 0)),
    )
    return pl.pallas_call(
        receiver_kernel,
        grid_spec=grid_spec,
        out_shape=jax.ShapeDtypeStruct((sector_count, rows, width), jnp.float32),
        compiler_params=pltpu.CompilerParams(vmem_limit_bytes=48 * 1024 * 1024),
    )(order, count, labels, incoming, right_env)


def term_exchange(partial_value, term_count):
    sector_count, rows, width = partial_value.shape
    pairs_count = term_count // 2
    pieces = partial_value.reshape(sector_count, pairs_count, 2, rows // term_count, width)
    mine = lax.axis_index("term")
    ring = mine // 2
    side = mine % 2
    keep = lax.dynamic_index_in_dim(pieces, side, axis=2, keepdims=False)
    away = lax.dynamic_index_in_dim(pieces, 1 - side, axis=2, keepdims=False)
    partner = [(dev, dev ^ 1) for dev in range(term_count)]
    merged = keep + lax.ppermute(away, "term", partner)
    total = lax.dynamic_index_in_dim(merged, ring, axis=1, keepdims=False)
    for shift in range(1, pairs_count):
        sent = lax.dynamic_index_in_dim(merged, (ring + shift) % pairs_count, axis=1, keepdims=False)
        pairs = [
            (dev, 2 * ((dev // 2 + shift) % pairs_count) + dev % 2) for dev in range(term_count)
        ]
        total = total + lax.ppermute(sent, "term", pairs)
    return total


def on_device(psi, left_env, right_env, target):
    term_count = lax.axis_size("term")
    slot_index, empty_slots, labels = slot_tables(target)
    labels_in = lax.all_to_all(labels, "sector", split_axis=0, concat_axis=0, tiled=True)
    results = []
    for half in range(SPLIT):
        piece_out = send_blocks(slot_index, empty_slots, left_env, psi, term_count, half)
        incoming = lax.all_to_all(piece_out, "sector", split_axis=0, concat_axis=0, tiled=True)
        partial_value = receive_blocks(labels_in, incoming, right_env)
        results.append(term_exchange(partial_value, term_count))
    return jnp.concatenate(results, axis=1)


def solution(mesh):
    in_specs = (
        P("sector", None, None),
        P("term", "sector", None, None),
        P("term", "sector", None, None),
        P("term", "sector"),
    )
    out_specs = P("sector", "term", None)
    return jax.shard_map(
        on_device, mesh=mesh, in_specs=in_specs, out_specs=out_specs, check_vma=False
    )
```

```python
import functools

import jax
import jax.numpy as jnp
from jax import lax
from jax.experimental import pallas as pl
from jax.experimental.pallas import tpu as pltpu
from jax.sharding import PartitionSpec as P


CAP = 4
GROUP = 8
SENDER_STEPS = 4
SPLIT = 2


def split_dot(a, b):
    rows = a.shape[0]
    a_hi = a.astype(jnp.bfloat16)
    a_lo = (a - a_hi.astype(jnp.float32)).astype(jnp.bfloat16)
    b_hi = b.astype(jnp.bfloat16)
    b_lo = (b - b_hi.astype(jnp.float32)).astype(jnp.bfloat16)
    both = jnp.dot(
        jnp.concatenate([a_hi, a_lo], axis=0), b_hi, preferred_element_type=jnp.float32
    )
    cross = jnp.dot(a_hi, b_lo, preferred_element_type=jnp.float32)
    return both[:rows] + (cross + both[rows:])


def slot_tables(target_part):
    term_count, sector_count = target_part.shape
    item_count = term_count * sector_count
    slot_count = lax.axis_size("sector") * CAP
    flat_target = target_part.reshape(item_count)
    owner_dev = flat_target // sector_count
    local_target = flat_target % sector_count
    item_index = jnp.arange(item_count, dtype=jnp.int32)
    term_index = item_index // sector_count
    earlier = (owner_dev[:, None] == owner_dev[None, :]) & (
        item_index[None, :] < item_index[:, None]
    )
    rank_slot = jnp.sum(earlier.astype(jnp.int32), axis=1)
    slot_index = jnp.minimum(owner_dev * CAP + rank_slot, slot_count - 1).astype(jnp.int32)
    slot_range = jnp.arange(slot_count, dtype=jnp.int32)
    match = slot_index[None, :] == slot_range[:, None]
    occupied = jnp.any(match, axis=1)
    item_of_slot = jnp.sum(jnp.where(match, item_index[None, :], 0), axis=1)
    label_of_item = term_index * sector_count + local_target + 1
    labels = jnp.where(occupied, label_of_item[item_of_slot], 0).astype(jnp.int32)
    return slot_index, compact_order(~occupied), labels


def compact_order(flags):
    count = flags.shape[0]
    first = jnp.cumsum(flags.astype(jnp.int32)) - 1
    rest = jnp.sum(flags.astype(jnp.int32)) + jnp.cumsum((~flags).astype(jnp.int32)) - 1
    position = jnp.where(flags, first, rest)
    spots = jnp.arange(count, dtype=jnp.int32)
    chosen = position[None, :] == spots[:, None]
    return jnp.sum(jnp.where(chosen, spots[None, :], 0), axis=1).astype(jnp.int32)


def sender_kernel(slot_ref, empty_ref, left_ref, psi_ref, out_ref, *, term_count, half):
    terms, sector_count = left_ref.shape[:2]
    width = psi_ref.shape[-1]
    band = width // term_count
    piece = band // SPLIT
    step = pl.program_id(0)
    per_step = sector_count // SENDER_STEPS

    @pl.when(step == 0)
    def _():
        for k in range(out_ref.shape[0] - terms * sector_count):
            out_ref[empty_ref[k]] = jnp.zeros(out_ref.shape[1:], jnp.float32)

    for j in range(per_step):
        source = step * per_step + j
        rows = jnp.concatenate(
            [
                left_ref[w, source, pl.ds(i * band + half * piece, piece), :]
                for w in range(terms)
                for i in range(term_count)
            ],
            axis=0,
        )
        value = split_dot(rows, psi_ref[source])
        for w in range(terms):
            out_ref[slot_ref[w * sector_count + source]] = value[w * piece * term_count:(w + 1) * piece * term_count]


def send_blocks(slot_index, empty_slots, left_env, psi, term_count, half):
    slot_count = empty_slots.shape[0]
    width = psi.shape[-1]
    rows = width // SPLIT
    grid_spec = pltpu.PrefetchScalarGridSpec(
        num_scalar_prefetch=2,
        grid=(SENDER_STEPS,),
        in_specs=[
            pl.BlockSpec(left_env.shape, lambda g, *_: (0, 0, 0, 0)),
            pl.BlockSpec(psi.shape, lambda g, *_: (0, 0, 0)),
        ],
        out_specs=pl.BlockSpec((slot_count, rows, width), lambda g, *_: (0, 0, 0)),
    )
    return pl.pallas_call(
        functools.partial(sender_kernel, term_count=term_count, half=half),
        grid_spec=grid_spec,
        out_shape=jax.ShapeDtypeStruct((slot_count, rows, width), jnp.float32),
        compiler_params=pltpu.CompilerParams(vmem_limit_bytes=48 * 1024 * 1024),
    )(slot_index, empty_slots, left_env, psi)


def receiver_kernel(order_ref, count_ref, label_ref, incoming_ref, right_ref, out_ref):
    sector_count = out_ref.shape[0]
    out_ref[...] = jnp.zeros(out_ref.shape, jnp.float32)

    def body(g, carry):
        targets = []
        values = []
        for j in range(GROUP):
            slot = order_ref[g * GROUP + j]
            pair = jnp.maximum(label_ref[slot] - 1, 0)
            term = pair // sector_count
            tgt = pair % sector_count
            targets.append(tgt)
            values.append(split_dot(incoming_ref[slot], right_ref[term, tgt]))
        for tgt, value in zip(targets, values):
            out_ref[tgt] += value
        return carry

    lax.fori_loop(0, (count_ref[0] + GROUP - 1) // GROUP, body, 0)


def receive_blocks(labels, incoming, right_env):
    sector_count = right_env.shape[1]
    _, rows, width = incoming.shape
    occupied = labels > 0
    order = compact_order(occupied)
    count = jnp.sum(occupied.astype(jnp.int32)).reshape(1)
    grid_spec = pltpu.PrefetchScalarGridSpec(
        num_scalar_prefetch=3,
        grid=(1,),
        in_specs=[
            pl.BlockSpec(incoming.shape, lambda g, *_: (0, 0, 0)),
            pl.BlockSpec(right_env.shape, lambda g, *_: (0, 0, 0, 0)),
        ],
        out_specs=pl.BlockSpec((sector_count, rows, width), lambda g, *_: (0, 0, 0)),
    )
    return pl.pallas_call(
        receiver_kernel,
        grid_spec=grid_spec,
        out_shape=jax.ShapeDtypeStruct((sector_count, rows, width), jnp.float32),
        compiler_params=pltpu.CompilerParams(vmem_limit_bytes=48 * 1024 * 1024),
    )(order, count, labels, incoming, right_env)


def term_exchange(partial_value, term_count):
    sector_count, rows, width = partial_value.shape
    pairs_count = term_count // 2
    pieces = partial_value.reshape(sector_count, pairs_count, 2, rows // term_count, width)
    mine = lax.axis_index("term")
    ring = mine // 2
    side = mine % 2
    keep = lax.dynamic_index_in_dim(pieces, side, axis=2, keepdims=False)
    away = lax.dynamic_index_in_dim(pieces, 1 - side, axis=2, keepdims=False)
    partner = [(dev, dev ^ 1) for dev in range(term_count)]
    merged = keep + lax.ppermute(away, "term", partner)
    total = lax.dynamic_index_in_dim(merged, ring, axis=1, keepdims=False)
    for shift in range(1, pairs_count):
        sent = lax.dynamic_index_in_dim(merged, (ring + shift) % pairs_count, axis=1, keepdims=False)
        pairs = [
            (dev, 2 * ((dev // 2 + shift) % pairs_count) + dev % 2) for dev in range(term_count)
        ]
        total = total + lax.ppermute(sent, "term", pairs)
    return total


def on_device_body(psi, left_env, right_env, target):
    term_count = lax.axis_size("term")
    slot_index, empty_slots, labels = slot_tables(target)
    labels_in = lax.all_to_all(labels, "sector", split_axis=0, concat_axis=0, tiled=True)
    results = []
    for half in range(SPLIT):
        piece_out = send_blocks(slot_index, empty_slots, left_env, psi, term_count, half)
        incoming = lax.all_to_all(piece_out, "sector", split_axis=0, concat_axis=0, tiled=True)
        partial_value = receive_blocks(labels_in, incoming, right_env)
        results.append(term_exchange(partial_value, term_count))
    return jnp.concatenate(results, axis=1)


def solution(mesh):
    in_specs = (
        P("sector", None, None),
        P("term", "sector", None, None),
        P("term", "sector", None, None),
        P("term", "sector"),
    )
    out_specs = P("sector", "term", None)
    return jax.shard_map(
        on_device_body, mesh=mesh, in_specs=in_specs, out_specs=out_specs, check_vma=False
    )
```

```python
import functools

import jax
import jax.numpy as jnp
from jax import lax
from jax.experimental import pallas as pl
from jax.experimental.pallas import tpu as pltpu
from jax.sharding import PartitionSpec as P


CAP = 4
GROUP = 8
SENDER_STEPS = 4
SPLIT = 2


def split_dot(a, b):
    rows = a.shape[0]
    a_hi = a.astype(jnp.bfloat16)
    a_lo = (a - a_hi.astype(jnp.float32)).astype(jnp.bfloat16)
    b_hi = b.astype(jnp.bfloat16)
    b_lo = (b - b_hi.astype(jnp.float32)).astype(jnp.bfloat16)
    both = jnp.dot(
        jnp.concatenate([a_hi, a_lo], axis=0), b_hi, preferred_element_type=jnp.float32
    )
    cross = jnp.dot(a_hi, b_lo, preferred_element_type=jnp.float32)
    return both[:rows] + (cross + both[rows:])


def slot_tables(target_part):
    term_count, sector_count = target_part.shape
    item_count = term_count * sector_count
    slot_count = lax.axis_size("sector") * CAP
    flat_target = target_part.reshape(item_count)
    owner_dev = flat_target // sector_count
    local_target = flat_target % sector_count
    item_index = jnp.arange(item_count, dtype=jnp.int32)
    term_index = item_index // sector_count
    earlier = (owner_dev[:, None] == owner_dev[None, :]) & (
        item_index[None, :] < item_index[:, None]
    )
    rank_slot = jnp.sum(earlier.astype(jnp.int32), axis=1)
    slot_index = jnp.minimum(owner_dev * CAP + rank_slot, slot_count - 1).astype(jnp.int32)
    slot_range = jnp.arange(slot_count, dtype=jnp.int32)
    match = slot_index[None, :] == slot_range[:, None]
    occupied = jnp.any(match, axis=1)
    item_of_slot = jnp.sum(jnp.where(match, item_index[None, :], 0), axis=1)
    label_of_item = term_index * sector_count + local_target + 1
    labels = jnp.where(occupied, label_of_item[item_of_slot], 0).astype(jnp.int32)
    return slot_index, compact_order(~occupied), labels


def compact_order(flags):
    count = flags.shape[0]
    first = jnp.cumsum(flags.astype(jnp.int32)) - 1
    rest = jnp.sum(flags.astype(jnp.int32)) + jnp.cumsum((~flags).astype(jnp.int32)) - 1
    position = jnp.where(flags, first, rest)
    spots = jnp.arange(count, dtype=jnp.int32)
    chosen = position[None, :] == spots[:, None]
    return jnp.sum(jnp.where(chosen, spots[None, :], 0), axis=1).astype(jnp.int32)


def sender_kernel(slot_ref, empty_ref, left_ref, psi_ref, out_ref, *, term_count, half):
    terms, sector_count = left_ref.shape[:2]
    width = psi_ref.shape[-1]
    band = width // term_count
    piece = band // SPLIT
    step = pl.program_id(0)
    per_step = sector_count // SENDER_STEPS

    @pl.when(step == 0)
    def _():
        for k in range(out_ref.shape[0] - terms * sector_count):
            out_ref[empty_ref[k]] = jnp.zeros(out_ref.shape[1:], jnp.float32)

    for j in range(per_step):
        source = step * per_step + j
        rows = jnp.concatenate(
            [
                left_ref[w, source, pl.ds(i * band + half * piece, piece), :]
                for w in range(terms)
                for i in range(term_count)
            ],
            axis=0,
        )
        value = split_dot(rows, psi_ref[source])
        for w in range(terms):
            out_ref[slot_ref[w * sector_count + source]] = value[w * piece * term_count:(w + 1) * piece * term_count]


def send_blocks(slot_index, empty_slots, left_env, psi, term_count, half):
    slot_count = empty_slots.shape[0]
    width = psi.shape[-1]
    rows = width // SPLIT
    grid_spec = pltpu.PrefetchScalarGridSpec(
        num_scalar_prefetch=2,
        grid=(SENDER_STEPS,),
        in_specs=[
            pl.BlockSpec(left_env.shape, lambda g, *_: (0, 0, 0, 0)),
            pl.BlockSpec(psi.shape, lambda g, *_: (0, 0, 0)),
        ],
        out_specs=pl.BlockSpec((slot_count, rows, width), lambda g, *_: (0, 0, 0)),
    )
    return pl.pallas_call(
        functools.partial(sender_kernel, term_count=term_count, half=half),
        grid_spec=grid_spec,
        out_shape=jax.ShapeDtypeStruct((slot_count, rows, width), jnp.float32),
        compiler_params=pltpu.CompilerParams(vmem_limit_bytes=48 * 1024 * 1024),
    )(slot_index, empty_slots, left_env, psi)


def receiver_kernel(order_ref, count_ref, label_ref, incoming_ref, right_ref, out_ref):
    sector_count = out_ref.shape[0]
    out_ref[...] = jnp.zeros(out_ref.shape, jnp.float32)

    def body(g, carry):
        targets = []
        values = []
        for j in range(GROUP):
            slot = order_ref[g * GROUP + j]
            pair = jnp.maximum(label_ref[slot] - 1, 0)
            term = pair // sector_count
            tgt = pair % sector_count
            targets.append(tgt)
            values.append(split_dot(incoming_ref[slot], right_ref[term, tgt]))
        for tgt, value in zip(targets, values):
            out_ref[tgt] += value
        return carry

    lax.fori_loop(0, (count_ref[0] + GROUP - 1) // GROUP, body, 0)


def receive_blocks(labels, incoming, right_env):
    sector_count = right_env.shape[1]
    _, rows, width = incoming.shape
    occupied = labels > 0
    order = compact_order(occupied)
    count = jnp.sum(occupied.astype(jnp.int32)).reshape(1)
    grid_spec = pltpu.PrefetchScalarGridSpec(
        num_scalar_prefetch=3,
        grid=(1,),
        in_specs=[
            pl.BlockSpec(incoming.shape, lambda g, *_: (0, 0, 0)),
            pl.BlockSpec(right_env.shape, lambda g, *_: (0, 0, 0, 0)),
        ],
        out_specs=pl.BlockSpec((sector_count, rows, width), lambda g, *_: (0, 0, 0)),
    )
    return pl.pallas_call(
        receiver_kernel,
        grid_spec=grid_spec,
        out_shape=jax.ShapeDtypeStruct((sector_count, rows, width), jnp.float32),
        compiler_params=pltpu.CompilerParams(vmem_limit_bytes=48 * 1024 * 1024),
    )(order, count, labels, incoming, right_env)


def term_exchange(partial_value, term_count):
    sector_count, rows, width = partial_value.shape
    pairs_count = term_count // 2
    pieces = partial_value.reshape(sector_count, pairs_count, 2, rows // term_count, width)
    mine = lax.axis_index("term")
    ring = mine // 2
    side = mine % 2
    keep = lax.dynamic_index_in_dim(pieces, side, axis=2, keepdims=False)
    away = lax.dynamic_index_in_dim(pieces, 1 - side, axis=2, keepdims=False)
    partner = [(dev, dev ^ 1) for dev in range(term_count)]
    merged = keep + lax.ppermute(away, "term", partner)
    total = lax.dynamic_index_in_dim(merged, ring, axis=1, keepdims=False)
    for shift in range(1, pairs_count):
        sent = lax.dynamic_index_in_dim(merged, (ring + shift) % pairs_count, axis=1, keepdims=False)
        pairs = [
            (dev, 2 * ((dev // 2 + shift) % pairs_count) + dev % 2) for dev in range(term_count)
        ]
        total = total + lax.ppermute(sent, "term", pairs)
    return total


def term_all_to_all(partial_value, term_count):
    sector_count, rows, width = partial_value.shape
    pieces = partial_value.reshape(sector_count, term_count, rows // term_count, width)
    pieces = pieces.transpose(1, 0, 2, 3)
    gathered = lax.all_to_all(pieces, "term", split_axis=0, concat_axis=0, tiled=True)
    return jnp.sum(gathered, axis=0)


def on_device_body(psi, left_env, right_env, target):
    term_count = lax.axis_size("term")
    slot_index, empty_slots, labels = slot_tables(target)
    labels_in = lax.all_to_all(labels, "sector", split_axis=0, concat_axis=0, tiled=True)
    results = []
    for half in range(SPLIT):
        piece_out = send_blocks(slot_index, empty_slots, left_env, psi, term_count, half)
        incoming = lax.all_to_all(piece_out, "sector", split_axis=0, concat_axis=0, tiled=True)
        partial_value = receive_blocks(labels_in, incoming, right_env)
        if half + 1 < SPLIT:
            results.append(term_exchange(partial_value, term_count))
        else:
            results.append(term_all_to_all(partial_value, term_count))
    return jnp.concatenate(results, axis=1)


def solution(mesh):
    in_specs = (
        P("sector", None, None),
        P("term", "sector", None, None),
        P("term", "sector", None, None),
        P("term", "sector"),
    )
    out_specs = P("sector", "term", None)
    return jax.shard_map(
        on_device_body, mesh=mesh, in_specs=in_specs, out_specs=out_specs, check_vma=False
    )
```

```python
import functools

import jax
import jax.numpy as jnp
from jax import lax
from jax.experimental import pallas as pl
from jax.experimental.pallas import tpu as pltpu
from jax.sharding import PartitionSpec as P


CAP = 4
GROUP = 8
SENDER_STEPS = 4
SPLIT = 2


def split_dot(a, b):
    rows = a.shape[0]
    a_hi = a.astype(jnp.bfloat16)
    a_lo = (a - a_hi.astype(jnp.float32)).astype(jnp.bfloat16)
    b_hi = b.astype(jnp.bfloat16)
    b_lo = (b - b_hi.astype(jnp.float32)).astype(jnp.bfloat16)
    both = jnp.dot(
        jnp.concatenate([a_hi, a_lo], axis=0), b_hi, preferred_element_type=jnp.float32
    )
    cross = jnp.dot(a_hi, b_lo, preferred_element_type=jnp.float32)
    return both[:rows] + (cross + both[rows:])


def slot_tables(target_part):
    term_count, sector_count = target_part.shape
    item_count = term_count * sector_count
    slot_count = lax.axis_size("sector") * CAP
    flat_target = target_part.reshape(item_count)
    owner_dev = flat_target // sector_count
    local_target = flat_target % sector_count
    item_index = jnp.arange(item_count, dtype=jnp.int32)
    term_index = item_index // sector_count
    earlier = (owner_dev[:, None] == owner_dev[None, :]) & (
        item_index[None, :] < item_index[:, None]
    )
    rank_slot = jnp.sum(earlier.astype(jnp.int32), axis=1)
    slot_index = jnp.minimum(owner_dev * CAP + rank_slot, slot_count - 1).astype(jnp.int32)
    slot_range = jnp.arange(slot_count, dtype=jnp.int32)
    match = slot_index[None, :] == slot_range[:, None]
    occupied = jnp.any(match, axis=1)
    item_of_slot = jnp.sum(jnp.where(match, item_index[None, :], 0), axis=1)
    label_of_item = term_index * sector_count + local_target + 1
    labels = jnp.where(occupied, label_of_item[item_of_slot], 0).astype(jnp.int32)
    return slot_index, compact_order(~occupied), labels


def compact_order(flags):
    count = flags.shape[0]
    first = jnp.cumsum(flags.astype(jnp.int32)) - 1
    rest = jnp.sum(flags.astype(jnp.int32)) + jnp.cumsum((~flags).astype(jnp.int32)) - 1
    position = jnp.where(flags, first, rest)
    spots = jnp.arange(count, dtype=jnp.int32)
    chosen = position[None, :] == spots[:, None]
    return jnp.sum(jnp.where(chosen, spots[None, :], 0), axis=1).astype(jnp.int32)


def sender_kernel(slot_ref, empty_ref, left_ref, psi_ref, *refs, term_count, half):
    out_ref = refs[-1]
    terms, sector_count = left_ref.shape[:2]
    width = psi_ref.shape[-1]
    band = width // term_count
    piece = band // SPLIT
    step = pl.program_id(0)
    per_step = sector_count // SENDER_STEPS

    def put(slot, value):
        out_ref[slot // CAP, pl.ds((slot % CAP) * piece * term_count, piece * term_count), :] = value

    @pl.when(step == 0)
    def _():
        for k in range(out_ref.shape[0] * CAP - terms * sector_count):
            put(empty_ref[k], jnp.zeros((piece * term_count, width), jnp.float32))
        if refs[:-1]:
            tiles_ref = refs[0]
            out_ref[:, pl.ds(CAP * piece * term_count, 8), :] = tiles_ref[...]

    for j in range(per_step):
        source = step * per_step + j
        rows = jnp.concatenate(
            [
                left_ref[w, source, pl.ds(i * band + half * piece, piece), :]
                for w in range(terms)
                for i in range(term_count)
            ],
            axis=0,
        )
        value = split_dot(rows, psi_ref[source])
        for w in range(terms):
            put(slot_ref[w * sector_count + source], value[w * piece * term_count:(w + 1) * piece * term_count])


def send_blocks(slot_index, empty_slots, left_env, psi, term_count, half, tiles):
    slot_count = empty_slots.shape[0]
    devices = slot_count // CAP
    width = psi.shape[-1]
    rows = width // SPLIT
    extra = [] if tiles is None else [tiles]
    height = CAP * rows + (0 if tiles is None else 8)
    grid_spec = pltpu.PrefetchScalarGridSpec(
        num_scalar_prefetch=2,
        grid=(SENDER_STEPS,),
        in_specs=[
            pl.BlockSpec(left_env.shape, lambda g, *_: (0, 0, 0, 0)),
            pl.BlockSpec(psi.shape, lambda g, *_: (0, 0, 0)),
        ]
        + [pl.BlockSpec(t.shape, lambda g, *_: (0, 0, 0)) for t in extra],
        out_specs=pl.BlockSpec((devices, height, width), lambda g, *_: (0, 0, 0)),
    )
    return pl.pallas_call(
        functools.partial(sender_kernel, term_count=term_count, half=half),
        grid_spec=grid_spec,
        out_shape=jax.ShapeDtypeStruct((devices, height, width), jnp.float32),
        compiler_params=pltpu.CompilerParams(vmem_limit_bytes=48 * 1024 * 1024),
    )(slot_index, empty_slots, left_env, psi, *extra)


def label_tiles(labels, width):
    devices = labels.shape[0] // CAP
    values = labels.reshape(devices, CAP).astype(jnp.float32)
    tiles = jnp.zeros((devices, 8, width), jnp.float32)
    return tiles.at[:, 0, :CAP].set(values)


def receiver_kernel(order_ref, count_ref, label_ref, incoming_ref, right_ref, out_ref):
    sector_count, rows = out_ref.shape[:2]
    out_ref[...] = jnp.zeros(out_ref.shape, jnp.float32)

    def body(g, carry):
        targets = []
        values = []
        for j in range(GROUP):
            slot = order_ref[g * GROUP + j]
            pair = jnp.maximum(label_ref[slot] - 1, 0)
            term = pair // sector_count
            tgt = pair % sector_count
            targets.append(tgt)
            block = incoming_ref[slot // CAP, pl.ds((slot % CAP) * rows, rows), :]
            values.append(split_dot(block, right_ref[term, tgt]))
        for tgt, value in zip(targets, values):
            out_ref[tgt] += value
        return carry

    lax.fori_loop(0, (count_ref[0] + GROUP - 1) // GROUP, body, 0)


def receive_blocks(labels, incoming, right_env):
    sector_count = right_env.shape[1]
    width = incoming.shape[-1]
    rows = right_env.shape[-1] // SPLIT
    occupied = labels > 0
    order = compact_order(occupied)
    count = jnp.sum(occupied.astype(jnp.int32)).reshape(1)
    grid_spec = pltpu.PrefetchScalarGridSpec(
        num_scalar_prefetch=3,
        grid=(1,),
        in_specs=[
            pl.BlockSpec(incoming.shape, lambda g, *_: (0, 0, 0)),
            pl.BlockSpec(right_env.shape, lambda g, *_: (0, 0, 0, 0)),
        ],
        out_specs=pl.BlockSpec((sector_count, rows, width), lambda g, *_: (0, 0, 0)),
    )
    return pl.pallas_call(
        receiver_kernel,
        grid_spec=grid_spec,
        out_shape=jax.ShapeDtypeStruct((sector_count, rows, width), jnp.float32),
        compiler_params=pltpu.CompilerParams(vmem_limit_bytes=48 * 1024 * 1024),
    )(order, count, labels, incoming, right_env)


def term_exchange(partial_value, term_count):
    sector_count, rows, width = partial_value.shape
    pairs_count = term_count // 2
    pieces = partial_value.reshape(sector_count, pairs_count, 2, rows // term_count, width)
    mine = lax.axis_index("term")
    ring = mine // 2
    side = mine % 2
    keep = lax.dynamic_index_in_dim(pieces, side, axis=2, keepdims=False)
    away = lax.dynamic_index_in_dim(pieces, 1 - side, axis=2, keepdims=False)
    partner = [(dev, dev ^ 1) for dev in range(term_count)]
    merged = keep + lax.ppermute(away, "term", partner)
    total = lax.dynamic_index_in_dim(merged, ring, axis=1, keepdims=False)
    for shift in range(1, pairs_count):
        sent = lax.dynamic_index_in_dim(merged, (ring + shift) % pairs_count, axis=1, keepdims=False)
        pairs = [
            (dev, 2 * ((dev // 2 + shift) % pairs_count) + dev % 2) for dev in range(term_count)
        ]
        total = total + lax.ppermute(sent, "term", pairs)
    return total


def term_all_to_all(partial_value, term_count):
    sector_count, rows, width = partial_value.shape
    pieces = partial_value.reshape(sector_count, term_count, rows // term_count, width)
    pieces = pieces.transpose(1, 0, 2, 3)
    gathered = lax.all_to_all(pieces, "term", split_axis=0, concat_axis=0, tiled=True)
    return jnp.sum(gathered, axis=0)


def on_device_body(psi, left_env, right_env, target):
    term_count = lax.axis_size("term")
    slot_index, empty_slots, labels = slot_tables(target)
    width = psi.shape[-1]
    tiles = label_tiles(labels, width)
    results = []
    labels_in = None
    for half in range(SPLIT):
        piece_out = send_blocks(slot_index, empty_slots, left_env, psi, term_count, half, tiles if half == 0 else None)
        incoming = lax.all_to_all(piece_out, "sector", split_axis=0, concat_axis=0, tiled=True)
        if labels_in is None:
            rows = width // SPLIT
            labels_in = incoming[:, CAP * rows, :CAP].astype(jnp.int32).reshape(-1)
        partial_value = receive_blocks(labels_in, incoming, right_env)
        if half + 1 < SPLIT:
            results.append(term_exchange(partial_value, term_count))
        else:
            results.append(term_all_to_all(partial_value, term_count))
    return jnp.concatenate(results, axis=1)


def solution(mesh):
    in_specs = (
        P("sector", None, None),
        P("term", "sector", None, None),
        P("term", "sector", None, None),
        P("term", "sector"),
    )
    out_specs = P("sector", "term", None)
    return jax.shard_map(on_device_body, mesh=mesh, in_specs=in_specs, out_specs=out_specs, check_vma=False)
```

```python
import functools

import jax
import jax.numpy as jnp
from jax import lax
from jax.experimental import pallas as pl
from jax.experimental.pallas import tpu as pltpu
from jax.sharding import PartitionSpec as P


CAP = 4
GROUP = 16
SENDER_STEPS = 1
SPLIT = 2


def split_dot(a, b):
    rows = a.shape[0]
    a_hi = a.astype(jnp.bfloat16)
    a_lo = (a - a_hi.astype(jnp.float32)).astype(jnp.bfloat16)
    b_hi = b.astype(jnp.bfloat16)
    b_lo = (b - b_hi.astype(jnp.float32)).astype(jnp.bfloat16)
    both = jnp.dot(
        jnp.concatenate([a_hi, a_lo], axis=0), b_hi, preferred_element_type=jnp.float32
    )
    cross = jnp.dot(a_hi, b_lo, preferred_element_type=jnp.float32)
    return both[:rows] + (cross + both[rows:])


def slot_tables(target_part):
    term_count, sector_count = target_part.shape
    item_count = term_count * sector_count
    slot_count = lax.axis_size("sector") * CAP
    flat_target = target_part.reshape(item_count)
    owner_dev = flat_target // sector_count
    local_target = flat_target % sector_count
    item_index = jnp.arange(item_count, dtype=jnp.int32)
    term_index = item_index // sector_count
    earlier = (owner_dev[:, None] == owner_dev[None, :]) & (
        item_index[None, :] < item_index[:, None]
    )
    rank_slot = jnp.sum(earlier.astype(jnp.int32), axis=1)
    slot_index = jnp.minimum(owner_dev * CAP + rank_slot, slot_count - 1).astype(jnp.int32)
    slot_range = jnp.arange(slot_count, dtype=jnp.int32)
    match = slot_index[None, :] == slot_range[:, None]
    occupied = jnp.any(match, axis=1)
    label_of_item = term_index * sector_count + local_target + 1
    labels = jnp.sum(jnp.where(match, label_of_item[None, :], 0), axis=1).astype(jnp.int32)
    return slot_index, compact_order(~occupied), labels


def compact_order(flags):
    count = flags.shape[0]
    first = jnp.cumsum(flags.astype(jnp.int32)) - 1
    rest = jnp.sum(flags.astype(jnp.int32)) + jnp.cumsum((~flags).astype(jnp.int32)) - 1
    position = jnp.where(flags, first, rest)
    spots = jnp.arange(count, dtype=jnp.int32)
    chosen = position[None, :] == spots[:, None]
    return jnp.sum(jnp.where(chosen, spots[None, :], 0), axis=1).astype(jnp.int32)


def sender_kernel(slot_ref, empty_ref, left_ref, psi_ref, *refs, term_count, half):
    out_ref = refs[-1]
    terms, sector_count = left_ref.shape[:2]
    width = psi_ref.shape[-1]
    band = width // term_count
    piece = band // SPLIT
    step = pl.program_id(0)
    per_step = sector_count // SENDER_STEPS

    def put(slot, value):
        out_ref[slot // CAP, pl.ds((slot % CAP) * piece * term_count, piece * term_count), :] = value

    @pl.when(step == 0)
    def _():
        for k in range(out_ref.shape[0] * CAP - terms * sector_count):
            put(empty_ref[k], jnp.zeros((piece * term_count, width), jnp.float32))
        if refs[:-1]:
            tiles_ref = refs[0]
            out_ref[:, pl.ds(CAP * piece * term_count, 8), :] = tiles_ref[...]

    for j in range(per_step):
        source = step * per_step + j
        rows = jnp.concatenate(
            [
                left_ref[w, source, pl.ds(i * band + half * piece, piece), :]
                for w in range(terms)
                for i in range(term_count)
            ],
            axis=0,
        )
        value = split_dot(rows, psi_ref[source])
        for w in range(terms):
            put(slot_ref[w * sector_count + source], value[w * piece * term_count:(w + 1) * piece * term_count])


def send_blocks(slot_index, empty_slots, left_env, psi, term_count, half, tiles):
    slot_count = empty_slots.shape[0]
    devices = slot_count // CAP
    width = psi.shape[-1]
    rows = width // SPLIT
    extra = [] if tiles is None else [tiles]
    height = CAP * rows + (0 if tiles is None else 8)
    grid_spec = pltpu.PrefetchScalarGridSpec(
        num_scalar_prefetch=2,
        grid=(SENDER_STEPS,),
        in_specs=[
            pl.BlockSpec(left_env.shape, lambda g, *_: (0, 0, 0, 0)),
            pl.BlockSpec(psi.shape, lambda g, *_: (0, 0, 0)),
        ]
        + [pl.BlockSpec(t.shape, lambda g, *_: (0, 0, 0)) for t in extra],
        out_specs=pl.BlockSpec((devices, height, width), lambda g, *_: (0, 0, 0)),
    )
    return pl.pallas_call(
        functools.partial(sender_kernel, term_count=term_count, half=half),
        grid_spec=grid_spec,
        out_shape=jax.ShapeDtypeStruct((devices, height, width), jnp.float32),
        compiler_params=pltpu.CompilerParams(vmem_limit_bytes=48 * 1024 * 1024),
    )(slot_index, empty_slots, left_env, psi, *extra)


def label_tiles(labels, width):
    devices = labels.shape[0] // CAP
    values = labels.reshape(devices, CAP).astype(jnp.float32)
    tiles = jnp.zeros((devices, 8, width), jnp.float32)
    return tiles.at[:, 0, :CAP].set(values)


def receiver_kernel(order_ref, count_ref, label_ref, incoming_ref, right_ref, out_ref):
    sector_count, rows = out_ref.shape[:2]
    out_ref[...] = jnp.zeros(out_ref.shape, jnp.float32)

    def body(g, carry):
        targets = []
        values = []
        for j in range(GROUP):
            slot = order_ref[g * GROUP + j]
            pair = jnp.maximum(label_ref[slot] - 1, 0)
            term = pair // sector_count
            tgt = pair % sector_count
            targets.append(tgt)
            block = incoming_ref[slot // CAP, pl.ds((slot % CAP) * rows, rows), :]
            values.append(split_dot(block, right_ref[term, tgt]))
        for tgt, value in zip(targets, values):
            out_ref[tgt] += value
        return carry

    lax.fori_loop(0, (count_ref[0] + GROUP - 1) // GROUP, body, 0)


def receive_blocks(labels, incoming, right_env):
    sector_count = right_env.shape[1]
    width = incoming.shape[-1]
    rows = right_env.shape[-1] // SPLIT
    occupied = labels > 0
    order = compact_order(occupied)
    count = jnp.sum(occupied.astype(jnp.int32)).reshape(1)
    grid_spec = pltpu.PrefetchScalarGridSpec(
        num_scalar_prefetch=3,
        grid=(1,),
        in_specs=[
            pl.BlockSpec(incoming.shape, lambda g, *_: (0, 0, 0)),
            pl.BlockSpec(right_env.shape, lambda g, *_: (0, 0, 0, 0)),
        ],
        out_specs=pl.BlockSpec((sector_count, rows, width), lambda g, *_: (0, 0, 0)),
    )
    return pl.pallas_call(
        receiver_kernel,
        grid_spec=grid_spec,
        out_shape=jax.ShapeDtypeStruct((sector_count, rows, width), jnp.float32),
        compiler_params=pltpu.CompilerParams(vmem_limit_bytes=48 * 1024 * 1024),
    )(order, count, labels, incoming, right_env)


def term_exchange(partial_value, term_count):
    sector_count, rows, width = partial_value.shape
    pairs_count = term_count // 2
    pieces = partial_value.reshape(sector_count, pairs_count, 2, rows // term_count, width)
    mine = lax.axis_index("term")
    ring = mine // 2
    side = mine % 2
    keep = lax.dynamic_index_in_dim(pieces, side, axis=2, keepdims=False)
    away = lax.dynamic_index_in_dim(pieces, 1 - side, axis=2, keepdims=False)
    partner = [(dev, dev ^ 1) for dev in range(term_count)]
    merged = keep + lax.ppermute(away, "term", partner)
    total = lax.dynamic_index_in_dim(merged, ring, axis=1, keepdims=False)
    for shift in range(1, pairs_count):
        sent = lax.dynamic_index_in_dim(merged, (ring + shift) % pairs_count, axis=1, keepdims=False)
        pairs = [
            (dev, 2 * ((dev // 2 + shift) % pairs_count) + dev % 2) for dev in range(term_count)
        ]
        total = total + lax.ppermute(sent, "term", pairs)
    return total


def term_all_to_all(partial_value, term_count):
    sector_count, rows, width = partial_value.shape
    pieces = partial_value.reshape(sector_count, term_count, rows // term_count, width)
    pieces = pieces.transpose(1, 0, 2, 3)
    gathered = lax.all_to_all(pieces, "term", split_axis=0, concat_axis=0, tiled=True)
    return jnp.sum(gathered, axis=0)


def on_device_body(psi, left_env, right_env, target):
    term_count = lax.axis_size("term")
    slot_index, empty_slots, labels = slot_tables(target)
    width = psi.shape[-1]
    tiles = label_tiles(labels, width)
    results = []
    labels_in = None
    for half in range(SPLIT):
        piece_out = send_blocks(slot_index, empty_slots, left_env, psi, term_count, half, tiles if half == 0 else None)
        incoming = lax.all_to_all(piece_out, "sector", split_axis=0, concat_axis=0, tiled=True)
        if labels_in is None:
            rows = width // SPLIT
            labels_in = incoming[:, CAP * rows, :CAP].astype(jnp.int32).reshape(-1)
        partial_value = receive_blocks(labels_in, incoming, right_env)
        if half + 1 < SPLIT:
            results.append(term_exchange(partial_value, term_count))
        else:
            results.append(term_all_to_all(partial_value, term_count))
    return jnp.concatenate(results, axis=1)


def solution(mesh):
    in_specs = (
        P("sector", None, None),
        P("term", "sector", None, None),
        P("term", "sector", None, None),
        P("term", "sector"),
    )
    out_specs = P("sector", "term", None)
    return jax.shard_map(on_device_body, mesh=mesh, in_specs=in_specs, out_specs=out_specs, check_vma=False)
```

```python
import functools

import jax
import jax.numpy as jnp
from jax import lax
from jax.experimental import pallas as pl
from jax.experimental.pallas import tpu as pltpu
from jax.sharding import PartitionSpec as P


CAP = 4
GROUP = 16
SENDER_STEPS = 1
SPLIT = 2


def split_dot(a, b):
    rows = a.shape[0]
    a_hi = a.astype(jnp.bfloat16)
    a_lo = (a - a_hi.astype(jnp.float32)).astype(jnp.bfloat16)
    b_hi = b.astype(jnp.bfloat16)
    b_lo = (b - b_hi.astype(jnp.float32)).astype(jnp.bfloat16)
    both = jnp.dot(
        jnp.concatenate([a_hi, a_lo], axis=0), b_hi, preferred_element_type=jnp.float32
    )
    cross = jnp.dot(a_hi, b_lo, preferred_element_type=jnp.float32)
    return both[:rows] + (cross + both[rows:])


def slot_tables(target_part):
    term_count, sector_count = target_part.shape
    item_count = term_count * sector_count
    slot_count = lax.axis_size("sector") * CAP
    flat_target = target_part.reshape(item_count)
    owner_dev = flat_target // sector_count
    local_target = flat_target % sector_count
    item_index = jnp.arange(item_count, dtype=jnp.int32)
    term_index = item_index // sector_count
    earlier = (owner_dev[:, None] == owner_dev[None, :]) & (
        item_index[None, :] < item_index[:, None]
    )
    rank_slot = jnp.sum(earlier.astype(jnp.int32), axis=1)
    slot_index = jnp.minimum(owner_dev * CAP + rank_slot, slot_count - 1).astype(jnp.int32)
    slot_range = jnp.arange(slot_count, dtype=jnp.int32)
    match = slot_index[None, :] == slot_range[:, None]
    occupied = jnp.any(match, axis=1)
    label_of_item = term_index * sector_count + local_target + 1
    labels = jnp.sum(jnp.where(match, label_of_item[None, :], 0), axis=1).astype(jnp.int32)
    return slot_index, compact_order(~occupied), labels


def compact_order(flags):
    count = flags.shape[0]
    first = jnp.cumsum(flags.astype(jnp.int32)) - 1
    rest = jnp.sum(flags.astype(jnp.int32)) + jnp.cumsum((~flags).astype(jnp.int32)) - 1
    position = jnp.where(flags, first, rest)
    spots = jnp.arange(count, dtype=jnp.int32)
    chosen = position[None, :] == spots[:, None]
    return jnp.sum(jnp.where(chosen, spots[None, :], 0), axis=1).astype(jnp.int32)


def sender_kernel(slot_ref, empty_ref, left_ref, psi_ref, *refs, term_count, half):
    out_ref = refs[-1]
    terms, sector_count = left_ref.shape[:2]
    width = psi_ref.shape[-1]
    band = width // term_count
    piece = band // SPLIT
    step = pl.program_id(0)
    per_step = sector_count // SENDER_STEPS

    def put(slot, value):
        out_ref[slot // CAP, pl.ds((slot % CAP) * piece * term_count, piece * term_count), :] = value

    @pl.when(step == 0)
    def _():
        for k in range(out_ref.shape[0] * CAP - terms * sector_count):
            put(empty_ref[k], jnp.zeros((piece * term_count, width), jnp.float32))
        if refs[:-1]:
            tiles_ref = refs[0]
            out_ref[:, pl.ds(CAP * piece * term_count, 8), :] = tiles_ref[...]

    for j in range(per_step):
        source = step * per_step + j
        rows = jnp.concatenate(
            [
                left_ref[w, source, pl.ds(i * band + half * piece, piece), :]
                for w in range(terms)
                for i in range(term_count)
            ],
            axis=0,
        )
        value = split_dot(rows, psi_ref[source])
        for w in range(terms):
            put(slot_ref[w * sector_count + source], value[w * piece * term_count:(w + 1) * piece * term_count])


def send_blocks(slot_index, empty_slots, left_env, psi, term_count, half, tiles):
    slot_count = empty_slots.shape[0]
    devices = slot_count // CAP
    width = psi.shape[-1]
    rows = width // SPLIT
    extra = [] if tiles is None else [tiles]
    height = CAP * rows + (0 if tiles is None else 8)
    grid_spec = pltpu.PrefetchScalarGridSpec(
        num_scalar_prefetch=2,
        grid=(SENDER_STEPS,),
        in_specs=[
            pl.BlockSpec(left_env.shape, lambda g, *_: (0, 0, 0, 0)),
            pl.BlockSpec(psi.shape, lambda g, *_: (0, 0, 0)),
        ]
        + [pl.BlockSpec(t.shape, lambda g, *_: (0, 0, 0)) for t in extra],
        out_specs=pl.BlockSpec((devices, height, width), lambda g, *_: (0, 0, 0)),
    )
    return pl.pallas_call(
        functools.partial(sender_kernel, term_count=term_count, half=half),
        grid_spec=grid_spec,
        out_shape=jax.ShapeDtypeStruct((devices, height, width), jnp.float32),
        compiler_params=pltpu.CompilerParams(vmem_limit_bytes=48 * 1024 * 1024),
    )(slot_index, empty_slots, left_env, psi, *extra)


def label_tiles(labels, width):
    devices = labels.shape[0] // CAP
    values = labels.reshape(devices, CAP).astype(jnp.float32)
    tiles = jnp.zeros((devices, 8, width), jnp.float32)
    return tiles.at[:, 0, :CAP].set(values)


def receiver_kernel(order_ref, count_ref, label_ref, incoming_ref, right_ref, out_ref):
    sector_count, rows = out_ref.shape[:2]
    out_ref[...] = jnp.zeros(out_ref.shape, jnp.float32)

    def body(g, carry):
        targets = []
        values = []
        for j in range(GROUP):
            slot = order_ref[g * GROUP + j]
            pair = jnp.maximum(label_ref[slot] - 1, 0)
            term = pair // sector_count
            tgt = pair % sector_count
            targets.append(tgt)
            block = incoming_ref[slot // CAP, pl.ds((slot % CAP) * rows, rows), :]
            values.append(split_dot(block, right_ref[term, tgt]))
        for tgt, value in zip(targets, values):
            out_ref[tgt] += value
        return carry

    lax.fori_loop(0, (count_ref[0] + GROUP - 1) // GROUP, body, 0)


def receive_blocks(labels, incoming, right_env):
    sector_count = right_env.shape[1]
    width = incoming.shape[-1]
    rows = right_env.shape[-1] // SPLIT
    occupied = labels > 0
    order = compact_order(occupied)
    count = jnp.sum(occupied.astype(jnp.int32)).reshape(1)
    grid_spec = pltpu.PrefetchScalarGridSpec(
        num_scalar_prefetch=3,
        grid=(1,),
        in_specs=[
            pl.BlockSpec(incoming.shape, lambda g, *_: (0, 0, 0)),
            pl.BlockSpec(right_env.shape, lambda g, *_: (0, 0, 0, 0)),
        ],
        out_specs=pl.BlockSpec((sector_count, rows, width), lambda g, *_: (0, 0, 0)),
    )
    return pl.pallas_call(
        receiver_kernel,
        grid_spec=grid_spec,
        out_shape=jax.ShapeDtypeStruct((sector_count, rows, width), jnp.float32),
        compiler_params=pltpu.CompilerParams(vmem_limit_bytes=48 * 1024 * 1024),
    )(order, count, labels, incoming, right_env)


def term_exchange_ring_first(partial_value, term_count):
    sector_count, rows, width = partial_value.shape
    pairs_count = term_count // 2
    pieces = partial_value.reshape(sector_count, pairs_count, 2, rows // term_count, width)
    mine = lax.axis_index("term")
    ring = mine // 2
    side = mine % 2
    merged = lax.dynamic_index_in_dim(pieces, ring, axis=1, keepdims=False)
    for shift in range(1, pairs_count):
        sent = lax.dynamic_index_in_dim(pieces, (ring + shift) % pairs_count, axis=1, keepdims=False)
        pairs = [
            (dev, 2 * ((dev // 2 + shift) % pairs_count) + dev % 2) for dev in range(term_count)
        ]
        merged = merged + lax.ppermute(sent, "term", pairs)
    keep = lax.dynamic_index_in_dim(merged, side, axis=1, keepdims=False)
    away = lax.dynamic_index_in_dim(merged, 1 - side, axis=1, keepdims=False)
    partner = [(dev, dev ^ 1) for dev in range(term_count)]
    return keep + lax.ppermute(away, "term", partner)


def on_device_body(psi, left_env, right_env, target):
    term_count = lax.axis_size("term")
    slot_index, empty_slots, labels = slot_tables(target)
    width = psi.shape[-1]
    tiles = label_tiles(labels, width)
    results = []
    labels_in = None
    for half in range(SPLIT):
        piece_out = send_blocks(slot_index, empty_slots, left_env, psi, term_count, half, tiles if half == 0 else None)
        incoming = lax.all_to_all(piece_out, "sector", split_axis=0, concat_axis=0, tiled=True)
        if labels_in is None:
            rows = width // SPLIT
            labels_in = incoming[:, CAP * rows, :CAP].astype(jnp.int32).reshape(-1)
        partial_value = receive_blocks(labels_in, incoming, right_env)
        results.append(term_exchange_ring_first(partial_value, term_count))
    return jnp.concatenate(results, axis=1)


def solution(mesh):
    in_specs = (
        P("sector", None, None),
        P("term", "sector", None, None),
        P("term", "sector", None, None),
        P("term", "sector"),
    )
    out_specs = P("sector", "term", None)
    return jax.shard_map(on_device_body, mesh=mesh, in_specs=in_specs, out_specs=out_specs, check_vma=False)
```

```python
import functools

import jax
import jax.numpy as jnp
from jax import lax
from jax.experimental import pallas as pl
from jax.experimental.pallas import tpu as pltpu
from jax.sharding import PartitionSpec as P


CAP = 4
GROUP = 8
SENDER_STEPS = 1
SPLIT = 2


def split_dot(a, b):
    rows = a.shape[0]
    a_hi = a.astype(jnp.bfloat16)
    a_lo = (a - a_hi.astype(jnp.float32)).astype(jnp.bfloat16)
    b_hi = b.astype(jnp.bfloat16)
    b_lo = (b - b_hi.astype(jnp.float32)).astype(jnp.bfloat16)
    both = jnp.dot(
        jnp.concatenate([a_hi, a_lo], axis=0), b_hi, preferred_element_type=jnp.float32
    )
    cross = jnp.dot(a_hi, b_lo, preferred_element_type=jnp.float32)
    return both[:rows] + (cross + both[rows:])


def slot_tables(target_part):
    term_count, sector_count = target_part.shape
    item_count = term_count * sector_count
    slot_count = lax.axis_size("sector") * CAP
    flat_target = target_part.reshape(item_count)
    owner_dev = flat_target // sector_count
    local_target = flat_target % sector_count
    item_index = jnp.arange(item_count, dtype=jnp.int32)
    term_index = item_index // sector_count
    earlier = (owner_dev[:, None] == owner_dev[None, :]) & (
        item_index[None, :] < item_index[:, None]
    )
    rank_slot = jnp.sum(earlier.astype(jnp.int32), axis=1)
    slot_index = jnp.minimum(owner_dev * CAP + rank_slot, slot_count - 1).astype(jnp.int32)
    slot_range = jnp.arange(slot_count, dtype=jnp.int32)
    match = slot_index[None, :] == slot_range[:, None]
    occupied = jnp.any(match, axis=1)
    label_of_item = term_index * sector_count + local_target + 1
    labels = jnp.sum(jnp.where(match, label_of_item[None, :], 0), axis=1).astype(jnp.int32)
    return slot_index, compact_order(~occupied), labels


def compact_order(flags):
    count = flags.shape[0]
    first = jnp.cumsum(flags.astype(jnp.int32)) - 1
    rest = jnp.sum(flags.astype(jnp.int32)) + jnp.cumsum((~flags).astype(jnp.int32)) - 1
    position = jnp.where(flags, first, rest)
    spots = jnp.arange(count, dtype=jnp.int32)
    chosen = position[None, :] == spots[:, None]
    return jnp.sum(jnp.where(chosen, spots[None, :], 0), axis=1).astype(jnp.int32)


def sender_kernel(slot_ref, empty_ref, left_ref, psi_ref, *refs, term_count, half):
    out_ref = refs[-1]
    terms, sector_count = left_ref.shape[:2]
    width = psi_ref.shape[-1]
    band = width // term_count
    piece = band // SPLIT
    step = pl.program_id(0)
    per_step = sector_count // SENDER_STEPS

    def put(slot, value):
        out_ref[slot // CAP, pl.ds((slot % CAP) * piece * term_count, piece * term_count), :] = value

    @pl.when(step == 0)
    def _():
        for k in range(out_ref.shape[0] * CAP - terms * sector_count):
            put(empty_ref[k], jnp.zeros((piece * term_count, width), jnp.float32))
        if refs[:-1]:
            tiles_ref = refs[0]
            out_ref[:, pl.ds(CAP * piece * term_count, 8), :] = tiles_ref[...]

    for j in range(per_step):
        source = step * per_step + j
        rows = jnp.concatenate(
            [
                left_ref[w, source, pl.ds(i * band + half * piece, piece), :]
                for w in range(terms)
                for i in range(term_count)
            ],
            axis=0,
        )
        value = split_dot(rows, psi_ref[source])
        for w in range(terms):
            put(slot_ref[w * sector_count + source], value[w * piece * term_count:(w + 1) * piece * term_count])


def send_blocks(slot_index, empty_slots, left_env, psi, term_count, half, tiles):
    slot_count = empty_slots.shape[0]
    devices = slot_count // CAP
    width = psi.shape[-1]
    rows = width // SPLIT
    extra = [] if tiles is None else [tiles]
    height = CAP * rows + (0 if tiles is None else 8)
    grid_spec = pltpu.PrefetchScalarGridSpec(
        num_scalar_prefetch=2,
        grid=(SENDER_STEPS,),
        in_specs=[
            pl.BlockSpec(left_env.shape, lambda g, *_: (0, 0, 0, 0)),
            pl.BlockSpec(psi.shape, lambda g, *_: (0, 0, 0)),
        ]
        + [pl.BlockSpec(t.shape, lambda g, *_: (0, 0, 0)) for t in extra],
        out_specs=pl.BlockSpec((devices, height, width), lambda g, *_: (0, 0, 0)),
    )
    return pl.pallas_call(
        functools.partial(sender_kernel, term_count=term_count, half=half),
        grid_spec=grid_spec,
        out_shape=jax.ShapeDtypeStruct((devices, height, width), jnp.float32),
        compiler_params=pltpu.CompilerParams(vmem_limit_bytes=48 * 1024 * 1024),
    )(slot_index, empty_slots, left_env, psi, *extra)


def label_tiles(labels, width):
    devices = labels.shape[0] // CAP
    values = labels.reshape(devices, CAP).astype(jnp.float32)
    tiles = jnp.zeros((devices, 8, width), jnp.float32)
    return tiles.at[:, 0, :CAP].set(values)


def receiver_kernel(order_ref, count_ref, label_ref, incoming_ref, right_ref, out_ref):
    sector_count, rows = out_ref.shape[:2]
    out_ref[...] = jnp.zeros(out_ref.shape, jnp.float32)

    def body(g, carry):
        targets = []
        values = []
        for j in range(GROUP):
            slot = order_ref[g * GROUP + j]
            pair = jnp.maximum(label_ref[slot] - 1, 0)
            term = pair // sector_count
            tgt = pair % sector_count
            targets.append(tgt)
            block = incoming_ref[slot // CAP, pl.ds((slot % CAP) * rows, rows), :]
            values.append(split_dot(block, right_ref[term, tgt]))
        for tgt, value in zip(targets, values):
            out_ref[tgt] += value
        return carry

    lax.fori_loop(0, (count_ref[0] + GROUP - 1) // GROUP, body, 0)


def receive_blocks(labels, incoming, right_env):
    sector_count = right_env.shape[1]
    width = incoming.shape[-1]
    rows = right_env.shape[-1] // SPLIT
    occupied = labels > 0
    order = compact_order(occupied)
    count = jnp.sum(occupied.astype(jnp.int32)).reshape(1)
    grid_spec = pltpu.PrefetchScalarGridSpec(
        num_scalar_prefetch=3,
        grid=(1,),
        in_specs=[
            pl.BlockSpec(incoming.shape, lambda g, *_: (0, 0, 0)),
            pl.BlockSpec(right_env.shape, lambda g, *_: (0, 0, 0, 0)),
        ],
        out_specs=pl.BlockSpec((sector_count, rows, width), lambda g, *_: (0, 0, 0)),
    )
    return pl.pallas_call(
        receiver_kernel,
        grid_spec=grid_spec,
        out_shape=jax.ShapeDtypeStruct((sector_count, rows, width), jnp.float32),
        compiler_params=pltpu.CompilerParams(vmem_limit_bytes=48 * 1024 * 1024),
    )(order, count, labels, incoming, right_env)


def term_exchange(partial_value, term_count):
    sector_count, rows, width = partial_value.shape
    pairs_count = term_count // 2
    pieces = partial_value.reshape(sector_count, pairs_count, 2, rows // term_count, width)
    mine = lax.axis_index("term")
    ring = mine // 2
    side = mine % 2
    keep = lax.dynamic_index_in_dim(pieces, side, axis=2, keepdims=False)
    away = lax.dynamic_index_in_dim(pieces, 1 - side, axis=2, keepdims=False)
    partner = [(dev, dev ^ 1) for dev in range(term_count)]
    merged = keep + lax.ppermute(away, "term", partner)
    total = lax.dynamic_index_in_dim(merged, ring, axis=1, keepdims=False)
    for shift in range(1, pairs_count):
        sent = lax.dynamic_index_in_dim(merged, (ring + shift) % pairs_count, axis=1, keepdims=False)
        pairs = [
            (dev, 2 * ((dev // 2 + shift) % pairs_count) + dev % 2) for dev in range(term_count)
        ]
        total = total + lax.ppermute(sent, "term", pairs)
    return total


def term_exchange_ring_first(partial_value, term_count):
    sector_count, rows, width = partial_value.shape
    pairs_count = term_count // 2
    pieces = partial_value.reshape(sector_count, pairs_count, 2, rows // term_count, width)
    mine = lax.axis_index("term")
    ring = mine // 2
    side = mine % 2
    merged = lax.dynamic_index_in_dim(pieces, ring, axis=1, keepdims=False)
    for shift in range(1, pairs_count):
        sent = lax.dynamic_index_in_dim(pieces, (ring + shift) % pairs_count, axis=1, keepdims=False)
        pairs = [
            (dev, 2 * ((dev // 2 + shift) % pairs_count) + dev % 2) for dev in range(term_count)
        ]
        merged = merged + lax.ppermute(sent, "term", pairs)
    keep = lax.dynamic_index_in_dim(merged, side, axis=1, keepdims=False)
    away = lax.dynamic_index_in_dim(merged, 1 - side, axis=1, keepdims=False)
    partner = [(dev, dev ^ 1) for dev in range(term_count)]
    return keep + lax.ppermute(away, "term", partner)


def on_device_body(psi, left_env, right_env, target):
    term_count = lax.axis_size("term")
    slot_index, empty_slots, labels = slot_tables(target)
    width = psi.shape[-1]
    tiles = label_tiles(labels, width)
    results = []
    labels_in = None
    for half in range(SPLIT):
        piece_out = send_blocks(slot_index, empty_slots, left_env, psi, term_count, half, tiles if half == 0 else None)
        incoming = lax.all_to_all(piece_out, "sector", split_axis=0, concat_axis=0, tiled=True)
        if labels_in is None:
            rows = width // SPLIT
            labels_in = incoming[:, CAP * rows, :CAP].astype(jnp.int32).reshape(-1)
        partial_value = receive_blocks(labels_in, incoming, right_env)
        if half + 1 < SPLIT:
            results.append(term_exchange(partial_value, term_count))
        else:
            results.append(term_exchange_ring_first(partial_value, term_count))
    return jnp.concatenate(results, axis=1)


def solution(mesh):
    in_specs = (
        P("sector", None, None),
        P("term", "sector", None, None),
        P("term", "sector", None, None),
        P("term", "sector"),
    )
    out_specs = P("sector", "term", None)
    return jax.shard_map(on_device_body, mesh=mesh, in_specs=in_specs, out_specs=out_specs, check_vma=False)
```
